256 devices in a mesh: cfg: 2 (over core), req: 16 (over x, y), tp: 8 (over z).
Axes of the slice: x: 4, y: 4, z: 8, core: 2. Of those that a mesh axis runs over, the one named last changes fastest.
Arguments:
- latent: float32 [6144, 64], P(('req', 'tp')), may hold values from -6 to 6
- states: float32 [2, 6144, 1536], P('cfg', ('req', 'tp')), may hold values from -12 to 12
- token_counts: int32 [3], replicated, may hold values from 1 to 3840, 6144 in all
- text_lens: int32 [2, 3], P('cfg'), may hold values from 1 to 512, 768 in all within a row
- steps_index: int32 [3], replicated, may hold values from 0 to 49
- modulation: float32 [3, 6, 1536], replicated, may hold values from -3 to 3
- self_qkv: bfloat16 [1536, 3, 2048], P(None, None, 'tp'), may hold values from -0.15625 to 0.15625
- self_out: bfloat16 [2048, 1536], P('tp'), may hold values from -0.15625 to 0.15625
- qk_gains: float32 [4, 2048], P(None, 'tp'), may hold values from 0.8 to 2
- cross_query: bfloat16 [1536, 2048], P(None, 'tp'), may hold values from -1 to 1
- cross_out: bfloat16 [2048, 1536], P('tp'), may hold values from -0.15625 to 0.15625
- cross_gain: float32 [1536], replicated, may hold values from 0.25 to 1.75
- text_kv: bfloat16 [2, 3, 2, 512, 2048], P('cfg', None, None, None, 'tp'), may hold values from -6 to 6
- ffn_in_weight: bfloat16 [8960, 1536], P(('cfg', 'tp')), may hold values from -0.15625 to 0.15625
- ffn_out_weight: bfloat16 [8960, 1536], P(('cfg', 'tp')), may hold values from -0.0625 to 0.0625
- head_weight: bfloat16 [1536, 64], replicated, may hold values from -0.15625 to 0.15625
Outputs:
- new_latent: float32 [6144, 64], P(('req', 'tp'), 'cfg')
- velocity: float32 [6144, 64], P(('req', 'tp'), 'cfg')
- peak: float32 [3], replicated
The draws below stay inside these ranges and needn't reach their ends.
Inputs may be any that keep to these rules, and one draw needn't show every extreme that they name: `token_counts`: the counts sum to 6144 and the largest is exactly 3840. `text_lens`: in each prompt half the counts sum to 768 and the largest is exactly 512.
All inputs are finite; a program needn't handle non-finite values.
Results may differ from the reference program's by a relative error of at most 0.03.
Values may be sent and summed in bfloat16 or wider, within the bound.
No kernel may reach another device: no remote copies, remote signals or barrier semaphores. Data moves between devices by JAX's collectives and lax.ppermute only.
A program may use at most 64 MiB of HBM per device.

```python
import math
import jax
import jax.numpy as jnp
import numpy as np
from jax import lax

D = 1536
HEADS = 12
HD = 128
FF = 8960
OUT = 64
TEXT = 512
REQS = 3
STEPS = 50
TOK_DEV = 384
HP = 16
TOKENS = 6144
MOST = 3840
N_CFG = 2
N_TP = 8


def draw_cross_query(key, part):
    width = HP * HD
    base = jax.random.normal(jax.random.fold_in(key, 11), (D, width), jnp.float32)
    base = jnp.clip(base, -5.0, 5.0)
    head_pos = (jnp.arange(width, dtype=jnp.int32) // HD).astype(jnp.float32)
    ratio = jnp.minimum(head_pos / (HEADS - 1.0), 1.0)
    column_scale = jnp.exp(-ratio * jnp.log(3.0))
    values = base * column_scale[None, :] * D ** (-0.5)
    return values.astype(jnp.bfloat16)


def draw_states(key, part):
    frac = jnp.arange(TOKENS, dtype=jnp.int32).astype(jnp.float32) / (TOKENS - 1.0)
    base = jnp.clip(jax.random.normal(jax.random.fold_in(key, 23), (TOKENS, D), jnp.float32), -5.0, 5.0)
    fresh = jnp.clip(jax.random.normal(jax.random.fold_in(key, 24), (TOKENS, D), jnp.float32), -5.0, 5.0)
    weight_rise = 0.05 * jnp.exp(frac * jnp.log(30.0))
    second = jnp.clip(base + weight_rise[:, None] * fresh, -12.0, 12.0)
    return jnp.stack([base, second]).astype(jnp.float32)


def block_levels(own_key, shape, pieces, smallest, top_value):
    def one(dim, blocks):
        steps = jax.random.uniform(jax.random.fold_in(jax.random.fold_in(own_key, 6), dim), (blocks,), jnp.float32, smallest / len(pieces), top_value / len(pieces))
        return jnp.repeat(jnp.exp(steps), shape[dim] // blocks).reshape((-1,) + (1,) * (len(shape) - dim - 1))

    level = one(*pieces[0])
    for cut in pieces[1:]:
        level = level * one(*cut)
    return level


def length_profile(count, total, most, lean):
    weights = [(1 << 20) // math.isqrt(standing ** lean) + 1 for standing in range(2, count + 1)]
    rest, holding = total - most - (count - 1), [1] * (count - 1)
    while rest > 0:
        free = [i for i in range(count - 1) if holding[i] < most]
        whole, budget = sum([weights[i] for i in free]), rest
        for i in free:
            extra = min(most - holding[i], max(1, budget * weights[i] // whole), rest)
            holding[i] = holding[i] + extra
            rest = rest - extra
    return np.array([most] + holding)


def uneven(rng, number_of, total, limit, skew):
    if number_of == 2:
        one = jax.random.randint(rng, (), max(1, total - limit), min(limit, total - 1) + 1)
        return jnp.stack([one, total - one])
    sizes = jnp.asarray(length_profile(number_of, total, limit, skew), jnp.int32)
    couples = (number_of - 1) // 2
    donor, taker = sizes[1:1 + 2 * couples:2], sizes[2:2 + 2 * couples:2]
    slack = jnp.minimum(donor - 1, limit - taker)
    shifted = jax.random.randint(jax.random.fold_in(rng, 1), (couples,), 0, 1 << 20) % (slack + 1)
    sizes = sizes.at[1:1 + 2 * couples:2].set(donor - shifted).at[2:2 + 2 * couples:2].set(taker + shifted)
    return sizes[jax.random.permutation(jax.random.fold_in(rng, 2), number_of)]


def normal_values(key, dims, scale, bound, shards=(), held_as=jnp.bfloat16):
    entries = jax.random.normal(key, dims, jnp.float32) * scale
    if len(shards) > 0:
        entries = block_levels(key, dims, shards, -0.22, 0.18) * entries
    return jnp.clip(entries, min=-bound, max=bound).astype(held_as)


def setup_inputs(seed: int = 0) -> dict:
    keys = jax.random.split(jax.random.key(seed), 17)
    return {
        "latent": normal_values(keys[0], (TOKENS, OUT), 1.0, 6.0, ((0, 128),), jnp.float32),
        "states": draw_states(jax.random.fold_in(keys[16], 71), 0),
        "token_counts": uneven(keys[2], REQS, TOKENS, MOST, 1).astype(jnp.int32),
        "text_lens": jax.vmap(lambda own: uneven(own, REQS, TEXT + TEXT // 2, TEXT, 1))(jax.random.split(keys[3], 2)).reshape((2, REQS)).astype(jnp.int32),
        "steps_index": jax.random.randint(keys[4], (REQS,), 0, STEPS).astype(jnp.int32),
        "modulation": normal_values(keys[5], (REQS, 6, D), 0.5, 3.0, (), jnp.float32),
        "self_qkv": normal_values(keys[6], (D, 3, HP * HD), D ** -0.5, 0.15625, ((2, 8),)),
        "self_out": normal_values(keys[7], (HP * HD, D), D ** -0.5, 0.15625, ((0, 8),)),
        "qk_gains": jnp.clip(jnp.exp(math.log(2.0) - 0.9162907 * jax.random.uniform(keys[8], (4, HP * HD), jnp.float32) ** block_levels(keys[8], (4, HP * HD), ((1, 8),), -0.2, 0.2)), 0.8, 2.0),
        "cross_query": draw_cross_query(jax.random.fold_in(keys[16], 71), 0),
        "cross_out": normal_values(keys[10], (HP * HD, D), D ** -0.5, 0.15625, ((0, 8),)),
        "cross_gain": jnp.clip(1.0 + 0.15 * jax.random.normal(keys[11], (D,), jnp.float32), 0.25, 1.75),
        "text_kv": normal_values(keys[12], (2, REQS, 2, TEXT, HP * HD), 1.0, 6.0, ((0, 2), (4, 8))),
        "ffn_in_weight": normal_values(keys[13], (FF, D), D ** -0.5, 0.15625, ((0, 16),)),
        "ffn_out_weight": normal_values(keys[14], (FF, D), FF ** -0.5, 0.0625, ((0, 16),)),
        "head_weight": normal_values(keys[15], (D, OUT), D ** -0.5, 0.15625),
    }


guide_scale = 5.0
rescale_mix = 0.7
flow_shift = 5.0
norm_eps = 1e-06
stat_eps = 1e-05

def layer_norm(values):
    average = lax.optimization_barrier(jnp.mean(values, axis=-1, keepdims=True))
    centered = values - average
    spread = lax.optimization_barrier(jnp.mean(centered * centered, axis=-1, keepdims=True))
    return centered * lax.rsqrt(spread + norm_eps)

def rms_norm(values, gains):
    real = values[:, :D]
    power = lax.optimization_barrier(jnp.mean(real * real, axis=1, keepdims=True))
    return (real * lax.rsqrt(power + norm_eps) * gains[:D]).astype(jnp.bfloat16)

def request_of(positions, request_ends):
    return lax.optimization_barrier(jnp.sum((positions[:, None] >= request_ends[None, :]).astype(jnp.int32), axis=1))

def presence(request_ids, request_count):
    return jnp.any(request_ids[:, None] == jnp.arange(request_count, dtype=jnp.int32)[None, :], axis=0)

def attend(running, queries, query_req, key_rows, value_rows, key_req, head_count, head_width):
    numerator, denominator = running
    query_count = queries.shape[0]
    key_count = key_rows.shape[0]
    query_wide = queries.astype(jnp.float32).reshape(query_count, head_count, head_width)
    key_wide = key_rows.astype(jnp.float32).reshape(key_count, head_count, head_width)
    scores = jnp.einsum('qhd,khd->hqk', query_wide, key_wide) * head_width ** (-0.5)
    same_req = query_req[:, None] == key_req[None, :]
    weights = jnp.where(same_req[None, :, :], jnp.exp(scores), 0.0)
    rounded = lax.optimization_barrier(weights.astype(jnp.bfloat16)).astype(jnp.float32)
    value_wide = value_rows.astype(jnp.float32).reshape(key_count, head_count, head_width)
    partial_sum = jnp.einsum('hqk,khd->qhd', rounded, value_wide)
    return (numerator + partial_sum.reshape(query_count, head_count * head_width), denominator + jnp.transpose(lax.optimization_barrier(jnp.sum(weights, axis=2))))

def finish_heads(running, head_count, head_width):
    numerator, denominator = running
    query_count = numerator.shape[0]
    mixed = numerator.reshape(query_count, head_count, head_width) / denominator[:, :, None]
    return mixed.reshape(query_count, head_count * head_width).astype(jnp.bfloat16)

def empty_state():
    return (jnp.zeros((TOK_DEV, D), jnp.float32), jnp.zeros((TOK_DEV, HEADS), jnp.float32))

def self_attention(queries, key_rows, value_rows, request_ids):
    blocks = TOKENS // TOK_DEV
    query_blocks = queries.reshape(blocks, TOK_DEV, D)
    key_blocks = key_rows.reshape(blocks, TOK_DEV, D)
    value_blocks = value_rows.reshape(blocks, TOK_DEV, D)
    request_blocks = request_ids.reshape(blocks, TOK_DEV)

    def per_block(inputs_pair):
        query_block, query_req = inputs_pair
        wanted = presence(query_req, REQS)

        def visit(running, key_inputs):
            key_block, value_block, key_req = key_inputs
            intersection = jnp.any(wanted & presence(key_req, REQS))

            def compute(current):
                return attend(current, query_block, query_req, key_block, value_block, key_req, HEADS, HD)

            def skip(current):
                return current
            return (lax.cond(intersection, compute, skip, running), None)
        final_state, unused = lax.scan(visit, empty_state(), (key_blocks, value_blocks, request_blocks))
        return finish_heads(final_state, HEADS, HD)
    return lax.map(per_block, (query_blocks, request_blocks)).reshape(TOKENS, D)

def cross_attention(queries, request_ids, text_half, lens_half, gains):
    blocks = TOKENS // TOK_DEV
    text_keys = rms_norm(text_half[:, 0].reshape(REQS * TEXT, HP * HD).astype(jnp.float32), gains)
    text_values = text_half[:, 1].reshape(REQS * TEXT, HP * HD)[:, :D]
    text_req = jnp.repeat(jnp.arange(REQS, dtype=jnp.int32), TEXT)
    text_pos = jnp.tile(jnp.arange(TEXT, dtype=jnp.int32), REQS)
    text_req = jnp.where(text_pos < lens_half[text_req], text_req, -1)

    def per_block(inputs_pair):
        query_block, query_req = inputs_pair
        final_state = attend(empty_state(), query_block, query_req, text_keys, text_values, text_req, HEADS, HD)
        return finish_heads(final_state, HEADS, HD)
    return lax.map(per_block, (queries.reshape(blocks, TOK_DEV, D), request_ids.reshape(blocks, TOK_DEV))).reshape(TOKENS, D)

def pad_heads(mixed):
    filler = jnp.zeros((mixed.shape[0], HP * HD - D), jnp.bfloat16)
    return jnp.concatenate([mixed, filler], axis=1)

def grouped_project(mixed, weight):
    group_cols = HP // N_TP * HD
    summed = jnp.zeros((mixed.shape[0], D), jnp.float32)
    for group_index in range(N_TP):
        lower = group_index * group_cols
        upper = lower + group_cols
        term = jnp.dot(mixed[:, lower:upper], weight[lower:upper], preferred_element_type=jnp.float32)
        summed = summed + lax.optimization_barrier(term.astype(jnp.bfloat16)).astype(jnp.float32)
    return summed

def feed_forward(rows, in_weight, out_weight):
    group_count = N_CFG * N_TP
    group_units = FF // group_count
    summed = jnp.zeros((rows.shape[0], D), jnp.float32)
    for group_index in range(group_count):
        lower = group_index * group_units
        upper = lower + group_units
        up_part = lax.dot_general(rows, in_weight[lower:upper], (((1,), (1,)), ((), ())), preferred_element_type=jnp.float32)
        activated = jax.nn.gelu(up_part, approximate=True).astype(jnp.bfloat16)
        term = jnp.dot(activated, out_weight[lower:upper], preferred_element_type=jnp.float32)
        summed = summed + lax.optimization_barrier(term.astype(jnp.bfloat16)).astype(jnp.float32)
    return summed

def request_mod(modulation, request_ids, which):
    return modulation[:, which][request_ids]

def noise_level(step_value):
    fraction = 1.0 - step_value / STEPS
    return flow_shift * fraction / (1.0 + (flow_shift - 1.0) * fraction)

def reference(latent, states, token_counts, text_lens, steps_index, modulation, self_qkv, self_out, qk_gains, cross_query, cross_out, cross_gain, text_kv, ffn_in_weight, ffn_out_weight, head_weight):
    request_ends = jnp.cumsum(token_counts).astype(jnp.int32)
    positions = jnp.arange(TOKENS, dtype=jnp.int32)
    request_ids = request_of(positions, request_ends)
    speeds = []
    for half in range(2):
        hidden_zero = states[half]
        normed = (layer_norm(hidden_zero) * (1.0 + request_mod(modulation, request_ids, 1)) + request_mod(modulation, request_ids, 0)).astype(jnp.bfloat16)
        query_proj = jnp.dot(normed, self_qkv[:, 0, :], preferred_element_type=jnp.float32)
        queries = rms_norm(query_proj, qk_gains[0])
        key_proj = jnp.dot(normed, self_qkv[:, 1, :], preferred_element_type=jnp.float32)
        key_rows = rms_norm(key_proj, qk_gains[1])
        value_proj = jnp.dot(normed, self_qkv[:, 2, :D], preferred_element_type=jnp.float32)
        value_rows = value_proj.astype(jnp.bfloat16)
        self_mix = pad_heads(self_attention(queries, key_rows, value_rows, request_ids))
        hidden_one = hidden_zero + request_mod(modulation, request_ids, 2) * grouped_project(self_mix, self_out)
        cross_in = (layer_norm(hidden_one) * cross_gain).astype(jnp.bfloat16)
        cross_proj = jnp.dot(cross_in, cross_query, preferred_element_type=jnp.float32)
        cross_q = rms_norm(cross_proj, qk_gains[2])
        cross_mix = pad_heads(cross_attention(cross_q, request_ids, text_kv[half], text_lens[half], qk_gains[3]))
        hidden_two = hidden_one + grouped_project(cross_mix, cross_out)
        ffn_in = (layer_norm(hidden_two) * (1.0 + request_mod(modulation, request_ids, 4)) + request_mod(modulation, request_ids, 3)).astype(jnp.bfloat16)
        hidden_three = hidden_two + request_mod(modulation, request_ids, 5) * feed_forward(ffn_in, ffn_in_weight, ffn_out_weight)
        speeds.append(jnp.dot(layer_norm(hidden_three).astype(jnp.bfloat16), head_weight, preferred_element_type=jnp.float32))
    cond_speed, plain_speed = speeds
    guided = plain_speed + guide_scale * (cond_speed - plain_speed)
    cond_sq = jax.ops.segment_sum(lax.optimization_barrier(jnp.sum(cond_speed * cond_speed, axis=1)), request_ids, REQS)
    guided_sq = jax.ops.segment_sum(lax.optimization_barrier(jnp.sum(guided * guided, axis=1)), request_ids, REQS)
    raw_peak = jax.ops.segment_max(lax.optimization_barrier(jnp.max(jnp.abs(guided), axis=1)), request_ids, REQS)
    entry_counts = token_counts.astype(jnp.float32) * OUT
    cond_rms = jnp.sqrt(cond_sq / entry_counts + stat_eps)
    guided_rms = jnp.sqrt(guided_sq / entry_counts + stat_eps)
    factor = rescale_mix * cond_rms / guided_rms + (1.0 - rescale_mix)
    step_value = steps_index.astype(jnp.float32)
    delta_t = noise_level(step_value + 1.0) - noise_level(step_value)
    velocity = factor[request_ids][:, None] * guided
    new_latent = latent + delta_t[request_ids][:, None] * velocity
    return (new_latent, velocity, factor * raw_peak)
```

```python
import jax
import jax.numpy as jnp
from jax import lax
from jax.sharding import PartitionSpec as P

HEADS = 12
HD = 128
STEPS = 50


key_block = 1024
guide_scale = 5.0
rescale_mix = 0.7
flow_shift = 5.0
norm_eps = 1e-06
stat_eps = 1e-05


def swapped(value, axis, stride):
    mask = 2**stride
    pairs = [(source, source ^ mask) for source in range(lax.axis_size(axis))]
    return lax.ppermute(value, axis, pairs)


def layer_norm(values):
    average = jnp.mean(values, axis=-1, keepdims=True)
    centered = values - average
    spread = jnp.mean(centered * centered, axis=-1, keepdims=True)
    return centered * lax.rsqrt(spread + norm_eps)


def rms_scale(values, square_sum, width, gains):
    return (values * lax.rsqrt(square_sum / width + norm_eps)[:, None] * gains).astype(jnp.bfloat16)


def request_of(positions, request_ends):
    return jnp.sum((positions[:, None] >= request_ends[None, :]).astype(jnp.int32), axis=1)


def presence(request_ids, request_count):
    return jnp.any(
        request_ids[:, None] == jnp.arange(request_count, dtype=jnp.int32)[None, :], axis=0
    )


def attend(running, queries, query_req, key_rows, value_rows, key_req, head_count, head_width):
    numerator, denominator = running
    query_count = queries.shape[0]
    key_count = key_rows.shape[0]
    scores = jnp.einsum(
        "qhd,khd->hqk",
        queries.reshape(query_count, head_count, head_width),
        key_rows.reshape(key_count, head_count, head_width),
        preferred_element_type=jnp.float32,
    ) * head_width ** (-0.5)
    same_req = query_req[:, None] == key_req[None, :]
    weights = jnp.where(same_req[None, :, :], jnp.exp(scores), 0.0)
    partial_sum = jnp.einsum(
        "hqk,khd->qhd",
        weights.astype(jnp.bfloat16),
        value_rows.reshape(key_count, head_count, head_width),
        preferred_element_type=jnp.float32,
    )
    return (
        numerator + partial_sum.reshape(query_count, head_count * head_width),
        denominator + jnp.transpose(jnp.sum(weights, axis=2)),
    )


def finish_heads(running, keep_cols, head_count, head_width):
    numerator, denominator = running
    query_count = numerator.shape[0]
    mixed = numerator.reshape(query_count, head_count, head_width) / denominator[:, :, None]
    return (mixed.reshape(query_count, head_count * head_width) * keep_cols).astype(jnp.bfloat16)


def fold_keys(
    running,
    queries,
    query_req,
    key_rows,
    value_rows,
    request_ends,
    all_tokens,
    head_count,
    head_width,
):
    key_total = key_rows.shape[0]
    request_count = request_ends.shape[0]
    wanted = presence(query_req, request_count)

    def visit_block(current, key_part, value_part, part_start):
        part_rows = key_part.shape[0]
        key_pos = part_start + jnp.arange(part_rows, dtype=jnp.int32)
        inside = (key_pos >= 0) & (key_pos < all_tokens)
        key_req = jnp.where(inside, request_of(key_pos, request_ends), -1)
        intersection = jnp.any(wanted & presence(key_req, request_count))

        def compute(state_now):
            return attend(
                state_now, queries, query_req, key_part, value_part, key_req, head_count, head_width
            )

        def skip(state_now):
            return state_now

        return lax.cond(intersection, compute, skip, current)

    full_blocks = key_total // key_block
    key_full = key_rows.reshape(full_blocks, key_block, key_rows.shape[1])
    value_full = value_rows.reshape(full_blocks, key_block, value_rows.shape[1])
    block_starts = key_block * jnp.arange(full_blocks, dtype=jnp.int32)

    def scan_step(current, block_inputs):
        return (visit_block(current, block_inputs[0], block_inputs[1], block_inputs[2]), None)

    running, unused = lax.scan(scan_step, running, (key_full, value_full, block_starts))
    return running


def gather_project(row_block, weight):
    return jnp.dot(
        lax.all_gather(row_block, "tp", axis=0, tiled=True),
        weight,
        preferred_element_type=jnp.float32,
    )


def scatter_project(mixed, weight):
    return lax.psum_scatter(
        jnp.dot(mixed, weight, preferred_element_type=jnp.float32).astype(jnp.bfloat16),
        "tp",
        scatter_dimension=0,
        tiled=True,
    ).astype(jnp.float32)


def feed_forward(ffn_rows, in_weight, out_weight):
    up_part = lax.dot_general(
        lax.all_gather(ffn_rows, ("cfg", "tp"), axis=0, tiled=True),
        in_weight,
        (((1,), (1,)), ((), ())),
        preferred_element_type=jnp.float32,
    )
    activated = jax.nn.gelu(up_part, approximate=True).astype(jnp.bfloat16)
    return lax.psum_scatter(
        jnp.dot(activated, out_weight, preferred_element_type=jnp.float32).astype(jnp.bfloat16),
        ("cfg", "tp"),
        scatter_dimension=0,
        tiled=True,
    ).astype(jnp.float32)


def noise_level(step_value):
    fraction = 1.0 - step_value / STEPS
    return flow_shift * fraction / (1.0 + (flow_shift - 1.0) * fraction)


def shards(
    latent,
    states,
    token_counts,
    text_lens,
    steps_index,
    modulation,
    self_qkv,
    self_out,
    qk_gains,
    cross_query,
    cross_out,
    cross_gain,
    text_kv,
    ffn_in_weight,
    ffn_out_weight,
    head_weight,
):
    row_count = latent.shape[0]
    head_width = HD
    local_cols = self_out.shape[0]
    head_count = local_cols // head_width
    model_width = head_weight.shape[0]
    request_count = token_counts.shape[0]
    tp_parts = lax.axis_size("tp")
    block_rows = row_count * tp_parts
    all_tokens = block_rows * lax.axis_size("req")
    request_ends = jnp.cumsum(token_counts)
    request_range = jnp.arange(request_count, dtype=jnp.int32)
    row_pos = (lax.axis_index("req") * tp_parts + lax.axis_index("tp")) * row_count + jnp.arange(
        row_count, dtype=jnp.int32
    )
    row_onehot = (request_of(row_pos, request_ends)[:, None] == request_range[None, :]).astype(
        jnp.float32
    )
    block_first = lax.axis_index("req") * block_rows
    query_req = request_of(block_first + jnp.arange(block_rows, dtype=jnp.int32), request_ends)
    head_ids = lax.axis_index("tp") * head_count + jnp.arange(head_count, dtype=jnp.int32)
    keep_cols = jnp.repeat((head_ids < HEADS).astype(jnp.float32), head_width)
    hidden_zero = states[0]
    text_local = text_kv[0]
    text_slots = text_local.shape[2]
    text_raw = (
        text_local[:, 0].reshape(request_count * text_slots, local_cols).astype(jnp.float32)
        * keep_cols
    )
    row_mods = jnp.dot(
        row_onehot,
        modulation.reshape(request_count, 6 * model_width),
        precision=lax.Precision.HIGHEST,
    )
    shift_attn = row_mods[:, :model_width]
    scale_attn = row_mods[:, model_width : 2 * model_width]
    gate_attn = row_mods[:, 2 * model_width : 3 * model_width]
    shift_ffn = row_mods[:, 3 * model_width : 4 * model_width]
    scale_ffn = row_mods[:, 4 * model_width : 5 * model_width]
    gate_ffn = row_mods[:, 5 * model_width :]
    normed = (layer_norm(hidden_zero) * (1.0 + scale_attn) + shift_attn).astype(jnp.bfloat16)
    projected = gather_project(normed, self_qkv.reshape(model_width, 3 * local_cols))
    query_raw = projected[:, :local_cols] * keep_cols
    key_raw = projected[:, local_cols : 2 * local_cols] * keep_cols
    query_sq, key_sq, text_sq = lax.psum(
        (
            jnp.sum(query_raw * query_raw, axis=1),
            jnp.sum(key_raw * key_raw, axis=1),
            jnp.sum(text_raw * text_raw, axis=1),
        ),
        "tp",
    )
    queries = rms_scale(query_raw, query_sq, model_width, qk_gains[0])
    key_rows = rms_scale(key_raw, key_sq, model_width, qk_gains[1])
    value_rows = projected[:, 2 * local_cols :].astype(jnp.bfloat16)
    kv_all = lax.all_gather(
        jnp.concatenate([key_rows, value_rows], axis=1), "req", axis=0, tiled=True
    )
    key_all = kv_all[:, :local_cols]
    value_all = kv_all[:, local_cols:]
    start_state = (
        jnp.zeros((block_rows, local_cols), jnp.float32),
        jnp.zeros((block_rows, head_count), jnp.float32),
    )
    running = fold_keys(
        start_state,
        queries,
        query_req,
        key_all,
        value_all,
        request_ends,
        all_tokens,
        head_count,
        head_width,
    )
    self_mix = finish_heads(running, keep_cols, head_count, head_width)
    hidden_one = hidden_zero + gate_attn * scatter_project(self_mix, self_out)
    cross_in = (layer_norm(hidden_one) * cross_gain).astype(jnp.bfloat16)
    cross_raw = gather_project(cross_in, cross_query) * keep_cols
    cross_sq = lax.psum(jnp.sum(cross_raw * cross_raw, axis=1), "tp")
    cross_q = rms_scale(cross_raw, cross_sq, model_width, qk_gains[2])
    text_keys = rms_scale(text_raw, text_sq, model_width, qk_gains[3])
    text_values = text_local[:, 1].reshape(request_count * text_slots, local_cols)
    text_req = jnp.repeat(request_range, text_slots)
    text_pos = jnp.tile(jnp.arange(text_slots, dtype=jnp.int32), request_count)
    text_limit = jnp.sum(
        jnp.where(text_req[:, None] == request_range[None, :], text_lens[0][None, :], 0), axis=1
    )
    text_req = jnp.where(text_pos < text_limit, text_req, -1)
    cross_state = attend(
        start_state, cross_q, query_req, text_keys, text_values, text_req, head_count, head_width
    )
    cross_mix = finish_heads(cross_state, keep_cols, head_count, head_width)
    hidden_two = hidden_one + scatter_project(cross_mix, cross_out)
    ffn_in = (layer_norm(hidden_two) * (1.0 + scale_ffn) + shift_ffn).astype(jnp.bfloat16)
    hidden_three = hidden_two + gate_ffn * feed_forward(ffn_in, ffn_in_weight, ffn_out_weight)
    velocity_own = jnp.dot(
        layer_norm(hidden_three).astype(jnp.bfloat16),
        head_weight,
        preferred_element_type=jnp.float32,
    )
    velocity_other = swapped(velocity_own, "cfg", 0)
    first_half = lax.axis_index("cfg") == 0
    cond_speed = jnp.where(first_half, velocity_own, velocity_other)
    plain_speed = jnp.where(first_half, velocity_other, velocity_own)
    guided = plain_speed + guide_scale * (cond_speed - plain_speed)
    row_squares = jnp.stack(
        [jnp.sum(cond_speed * cond_speed, axis=1), jnp.sum(guided * guided, axis=1)], axis=1
    )
    square_sums = jnp.dot(jnp.transpose(row_onehot), row_squares, precision=lax.Precision.HIGHEST)
    peak_speed = jnp.max(row_onehot * jnp.max(jnp.abs(guided), axis=1)[:, None], axis=0)
    slot_count = lax.axis_size("req") * tp_parts
    slot = lax.axis_index("req") * tp_parts + lax.axis_index("tp")
    peak_slots = jnp.where(
        (jnp.arange(slot_count, dtype=jnp.int32) == slot)[:, None], peak_speed[None, :], 0.0
    )
    packed = jnp.concatenate([square_sums.reshape(-1), peak_slots.reshape(-1)])
    packed = lax.psum(jnp.where(lax.axis_index("cfg") == 0, packed, 0.0), ("cfg", "req", "tp"))
    square_sums = packed[: 2 * request_count].reshape(request_count, 2)
    peak_speed = jnp.max(packed[2 * request_count :].reshape(slot_count, request_count), axis=0)
    entry_counts = token_counts.astype(jnp.float32) * guided.shape[1]
    cond_rms = jnp.sqrt(square_sums[:, 0] / entry_counts + stat_eps)
    guided_rms = jnp.sqrt(square_sums[:, 1] / entry_counts + stat_eps)
    factor = rescale_mix * cond_rms / guided_rms + (1.0 - rescale_mix)
    step_value = steps_index.astype(jnp.float32)
    delta_t = noise_level(step_value + 1.0) - noise_level(step_value)
    per_row = jnp.dot(
        row_onehot, jnp.stack([factor, delta_t], axis=1), precision=lax.Precision.HIGHEST
    )
    velocity = per_row[:, 0:1] * guided
    new_latent = latent + per_row[:, 1:2] * velocity
    own_cols = guided.shape[1] // lax.axis_size("cfg")
    col_start = lax.axis_index("cfg") * own_cols
    velocity_part = lax.dynamic_slice_in_dim(velocity, col_start, own_cols, 1)
    latent_part = lax.dynamic_slice_in_dim(new_latent, col_start, own_cols, 1)
    return (latent_part, velocity_part, factor * peak_speed)


def solution(mesh):
    in_specs = (
        P(("req", "tp"), None),
        P("cfg", ("req", "tp"), None),
        P(),
        P("cfg", None),
        P(),
        P(),
        P(None, None, "tp"),
        P("tp", None),
        P(None, "tp"),
        P(None, "tp"),
        P("tp", None),
        P(),
        P("cfg", None, None, None, "tp"),
        P(("cfg", "tp"), None),
        P(("cfg", "tp"), None),
        P(),
    )
    out_specs = (P(("req", "tp"), "cfg"), P(("req", "tp"), "cfg"), P())
    return jax.shard_map(shards, mesh=mesh, in_specs=in_specs, out_specs=out_specs, check_vma=False)
```

```python
import jax
import jax.numpy as jnp
from jax import lax
from jax.sharding import PartitionSpec as P

HEADS = 12
HD = 128
STEPS = 50


key_block = 1024
guide_scale = 5.0
rescale_mix = 0.7
flow_shift = 5.0
norm_eps = 1e-06
stat_eps = 1e-05


def swapped(value, axis, stride):
    mask = 2**stride
    pairs = [(source, source ^ mask) for source in range(lax.axis_size(axis))]
    return lax.ppermute(value, axis, pairs)


def shifted(value, axis, step):
    size = lax.axis_size(axis)
    return lax.ppermute(value, axis, [(source, (source + step) % size) for source in range(size)])


def ring_gather(value, axis):
    size = lax.axis_size(axis)
    forward, backward = value, value
    ahead, behind = [], []
    for unused in range(size // 2):
        forward = shifted(forward, axis, 1)
        behind.append(forward)
    for unused in range((size - 1) // 2):
        backward = shifted(backward, axis, -1)
        ahead.append(backward)
    by_offset = jnp.stack([value] + ahead + behind[::-1])
    doubled = jnp.concatenate([by_offset, by_offset], axis=0)
    start = (size - lax.axis_index(axis)) % size
    ordered = lax.dynamic_slice_in_dim(doubled, start, size, axis=0)
    return ordered.reshape((size * value.shape[0],) + value.shape[1:])


def scatter_sum(value, axis):
    size = lax.axis_size(axis)
    me = lax.axis_index(axis)
    blocks = value.reshape((size, value.shape[0] // size) + value.shape[1:])
    total = lax.dynamic_index_in_dim(blocks, me, 0, keepdims=False).astype(jnp.float32)
    for step in range(1, size):
        outgoing = lax.dynamic_index_in_dim(blocks, (me + step) % size, 0, keepdims=False)
        total = total + shifted(outgoing, axis, step).astype(jnp.float32)
    return total


def butterfly_sum(value, axis):
    stride = 1
    while stride < lax.axis_size(axis):
        value = value + swapped(value, axis, stride.bit_length() - 1)
        stride *= 2
    return value


def layer_norm(values):
    average = jnp.mean(values, axis=-1, keepdims=True)
    centered = values - average
    spread = jnp.mean(centered * centered, axis=-1, keepdims=True)
    return centered * lax.rsqrt(spread + norm_eps)


def rms_scale(values, square_sum, width, gains):
    return (values * lax.rsqrt(square_sum / width + norm_eps)[:, None] * gains).astype(jnp.bfloat16)


def request_of(positions, request_ends):
    return jnp.sum((positions[:, None] >= request_ends[None, :]).astype(jnp.int32), axis=1)


def presence(request_ids, request_count):
    return jnp.any(
        request_ids[:, None] == jnp.arange(request_count, dtype=jnp.int32)[None, :], axis=0
    )


def attend(running, queries, query_req, key_rows, value_rows, key_req, head_count, head_width):
    numerator, denominator = running
    query_count = queries.shape[0]
    key_count = key_rows.shape[0]
    scores = jnp.einsum(
        "qhd,khd->hqk",
        queries.reshape(query_count, head_count, head_width),
        key_rows.reshape(key_count, head_count, head_width),
        preferred_element_type=jnp.float32,
    ) * head_width ** (-0.5)
    same_req = query_req[:, None] == key_req[None, :]
    weights = jnp.where(same_req[None, :, :], jnp.exp(scores), 0.0)
    partial_sum = jnp.einsum(
        "hqk,khd->qhd",
        weights.astype(jnp.bfloat16),
        value_rows.reshape(key_count, head_count, head_width),
        preferred_element_type=jnp.float32,
    )
    return (
        numerator + partial_sum.reshape(query_count, head_count * head_width),
        denominator + jnp.transpose(jnp.sum(weights, axis=2)),
    )


def finish_heads(running, keep_cols, head_count, head_width):
    numerator, denominator = running
    query_count = numerator.shape[0]
    mixed = numerator.reshape(query_count, head_count, head_width) / denominator[:, :, None]
    return (mixed.reshape(query_count, head_count * head_width) * keep_cols).astype(jnp.bfloat16)


def fold_keys(
    running,
    queries,
    query_req,
    key_rows,
    value_rows,
    request_ends,
    all_tokens,
    head_count,
    head_width,
):
    key_total = key_rows.shape[0]
    request_count = request_ends.shape[0]
    wanted = presence(query_req, request_count)

    def visit_block(current, key_part, value_part, part_start):
        part_rows = key_part.shape[0]
        key_pos = part_start + jnp.arange(part_rows, dtype=jnp.int32)
        inside = (key_pos >= 0) & (key_pos < all_tokens)
        key_req = jnp.where(inside, request_of(key_pos, request_ends), -1)
        intersection = jnp.any(wanted & presence(key_req, request_count))

        def compute(state_now):
            return attend(
                state_now, queries, query_req, key_part, value_part, key_req, head_count, head_width
            )

        def skip(state_now):
            return state_now

        return lax.cond(intersection, compute, skip, current)

    full_blocks = key_total // key_block
    key_full = key_rows.reshape(full_blocks, key_block, key_rows.shape[1])
    value_full = value_rows.reshape(full_blocks, key_block, value_rows.shape[1])
    block_starts = key_block * jnp.arange(full_blocks, dtype=jnp.int32)

    def scan_step(current, block_inputs):
        return (visit_block(current, block_inputs[0], block_inputs[1], block_inputs[2]), None)

    running, unused = lax.scan(scan_step, running, (key_full, value_full, block_starts))
    return running


def gather_project(row_block, weight):
    return jnp.dot(ring_gather(row_block, "tp"), weight, preferred_element_type=jnp.float32)


def scatter_project(mixed, weight):
    return scatter_sum(
        jnp.dot(mixed, weight, preferred_element_type=jnp.float32).astype(jnp.bfloat16), "tp"
    )


def feed_forward(ffn_rows, in_weight, out_weight):
    partner_in, partner_out = swapped((in_weight, out_weight), "cfg", 0)
    units = in_weight.shape[0]
    rows = ring_gather(ffn_rows, "tp")
    up_part = lax.dot_general(
        rows,
        jnp.concatenate([in_weight, partner_in], axis=0),
        (((1,), (1,)), ((), ())),
        preferred_element_type=jnp.float32,
    )
    activated = jax.nn.gelu(up_part, approximate=True).astype(jnp.bfloat16)
    own_term = jnp.dot(activated[:, :units], out_weight, preferred_element_type=jnp.float32)
    partner_term = jnp.dot(activated[:, units:], partner_out, preferred_element_type=jnp.float32)
    pair = own_term.astype(jnp.bfloat16).astype(jnp.float32) + partner_term.astype(
        jnp.bfloat16
    ).astype(jnp.float32)
    return scatter_sum(pair.astype(jnp.bfloat16), "tp")


def noise_level(step_value):
    fraction = 1.0 - step_value / STEPS
    return flow_shift * fraction / (1.0 + (flow_shift - 1.0) * fraction)


def shards(
    latent,
    states,
    token_counts,
    text_lens,
    steps_index,
    modulation,
    self_qkv,
    self_out,
    qk_gains,
    cross_query,
    cross_out,
    cross_gain,
    text_kv,
    ffn_in_weight,
    ffn_out_weight,
    head_weight,
):
    row_count = latent.shape[0]
    head_width = HD
    local_cols = self_out.shape[0]
    head_count = local_cols // head_width
    model_width = head_weight.shape[0]
    request_count = token_counts.shape[0]
    tp_parts = lax.axis_size("tp")
    block_rows = row_count * tp_parts
    all_tokens = block_rows * lax.axis_size("req")
    request_ends = jnp.cumsum(token_counts)
    request_range = jnp.arange(request_count, dtype=jnp.int32)
    row_pos = (lax.axis_index("req") * tp_parts + lax.axis_index("tp")) * row_count + jnp.arange(
        row_count, dtype=jnp.int32
    )
    row_onehot = (request_of(row_pos, request_ends)[:, None] == request_range[None, :]).astype(
        jnp.float32
    )
    block_first = lax.axis_index("req") * block_rows
    query_req = request_of(block_first + jnp.arange(block_rows, dtype=jnp.int32), request_ends)
    head_ids = lax.axis_index("tp") * head_count + jnp.arange(head_count, dtype=jnp.int32)
    keep_cols = jnp.repeat((head_ids < HEADS).astype(jnp.float32), head_width)
    hidden_zero = states[0]
    text_local = text_kv[0]
    text_slots = text_local.shape[2]
    text_raw = (
        text_local[:, 0].reshape(request_count * text_slots, local_cols).astype(jnp.float32)
        * keep_cols
    )
    text_sq = butterfly_sum(jnp.sum(text_raw * text_raw, axis=1), "tp")
    row_mods = jnp.dot(
        row_onehot,
        modulation.reshape(request_count, 6 * model_width),
        precision=lax.Precision.HIGHEST,
    )
    shift_attn = row_mods[:, :model_width]
    scale_attn = row_mods[:, model_width : 2 * model_width]
    gate_attn = row_mods[:, 2 * model_width : 3 * model_width]
    shift_ffn = row_mods[:, 3 * model_width : 4 * model_width]
    scale_ffn = row_mods[:, 4 * model_width : 5 * model_width]
    gate_ffn = row_mods[:, 5 * model_width :]
    normed = (layer_norm(hidden_zero) * (1.0 + scale_attn) + shift_attn).astype(jnp.bfloat16)
    projected = gather_project(normed, self_qkv.reshape(model_width, 3 * local_cols))
    query_raw = projected[:, :local_cols] * keep_cols
    key_raw = projected[:, local_cols : 2 * local_cols] * keep_cols
    query_sq = butterfly_sum(jnp.sum(query_raw * query_raw, axis=1), "tp")
    key_sq = butterfly_sum(jnp.sum(key_raw * key_raw, axis=1), "tp")
    queries = rms_scale(query_raw, query_sq, model_width, qk_gains[0])
    key_rows = rms_scale(key_raw, key_sq, model_width, qk_gains[1])
    value_rows = projected[:, 2 * local_cols :].astype(jnp.bfloat16)
    kv_all = lax.all_gather(
        jnp.concatenate([key_rows, value_rows], axis=1), "req", axis=0, tiled=True
    )
    key_all = kv_all[:, :local_cols]
    value_all = kv_all[:, local_cols:]
    start_state = (
        jnp.zeros((block_rows, local_cols), jnp.float32),
        jnp.zeros((block_rows, head_count), jnp.float32),
    )
    running = fold_keys(
        start_state,
        queries,
        query_req,
        key_all,
        value_all,
        request_ends,
        all_tokens,
        head_count,
        head_width,
    )
    self_mix = finish_heads(running, keep_cols, head_count, head_width)
    hidden_one = hidden_zero + gate_attn * scatter_project(self_mix, self_out)
    cross_in = (layer_norm(hidden_one) * cross_gain).astype(jnp.bfloat16)
    cross_raw = gather_project(cross_in, cross_query) * keep_cols
    cross_sq = butterfly_sum(jnp.sum(cross_raw * cross_raw, axis=1), "tp")
    cross_q = rms_scale(cross_raw, cross_sq, model_width, qk_gains[2])
    text_keys = rms_scale(text_raw, text_sq, model_width, qk_gains[3])
    text_values = text_local[:, 1].reshape(request_count * text_slots, local_cols)
    text_req = jnp.repeat(request_range, text_slots)
    text_pos = jnp.tile(jnp.arange(text_slots, dtype=jnp.int32), request_count)
    text_limit = jnp.sum(
        jnp.where(text_req[:, None] == request_range[None, :], text_lens[0][None, :], 0), axis=1
    )
    text_req = jnp.where(text_pos < text_limit, text_req, -1)
    cross_state = attend(
        start_state, cross_q, query_req, text_keys, text_values, text_req, head_count, head_width
    )
    cross_mix = finish_heads(cross_state, keep_cols, head_count, head_width)
    hidden_two = hidden_one + scatter_project(cross_mix, cross_out)
    ffn_in = (layer_norm(hidden_two) * (1.0 + scale_ffn) + shift_ffn).astype(jnp.bfloat16)
    hidden_three = hidden_two + gate_ffn * feed_forward(ffn_in, ffn_in_weight, ffn_out_weight)
    velocity_own = jnp.dot(
        layer_norm(hidden_three).astype(jnp.bfloat16),
        head_weight,
        preferred_element_type=jnp.float32,
    )
    velocity_other = swapped(velocity_own, "cfg", 0)
    first_half = lax.axis_index("cfg") == 0
    cond_speed = jnp.where(first_half, velocity_own, velocity_other)
    plain_speed = jnp.where(first_half, velocity_other, velocity_own)
    guided = plain_speed + guide_scale * (cond_speed - plain_speed)
    row_squares = jnp.stack(
        [jnp.sum(cond_speed * cond_speed, axis=1), jnp.sum(guided * guided, axis=1)], axis=1
    )
    square_sums = jnp.dot(jnp.transpose(row_onehot), row_squares, precision=lax.Precision.HIGHEST)
    peak_speed = jnp.max(row_onehot * jnp.max(jnp.abs(guided), axis=1)[:, None], axis=0)
    packed = jnp.concatenate([square_sums.reshape(-1), peak_speed])
    sum_count = 2 * request_count
    for axis in ("tp", "req"):
        stride = 1
        while stride < lax.axis_size(axis):
            other = swapped(packed, axis, stride.bit_length() - 1)
            packed = jnp.concatenate(
                [packed[:sum_count] + other[:sum_count], jnp.maximum(packed[sum_count:], other[sum_count:])]
            )
            stride *= 2
    square_sums = packed[:sum_count].reshape(request_count, 2)
    peak_speed = packed[sum_count:]
    entry_counts = token_counts.astype(jnp.float32) * guided.shape[1]
    cond_rms = jnp.sqrt(square_sums[:, 0] / entry_counts + stat_eps)
    guided_rms = jnp.sqrt(square_sums[:, 1] / entry_counts + stat_eps)
    factor = rescale_mix * cond_rms / guided_rms + (1.0 - rescale_mix)
    step_value = steps_index.astype(jnp.float32)
    delta_t = noise_level(step_value + 1.0) - noise_level(step_value)
    per_row = jnp.dot(
        row_onehot, jnp.stack([factor, delta_t], axis=1), precision=lax.Precision.HIGHEST
    )
    velocity = per_row[:, 0:1] * guided
    new_latent = latent + per_row[:, 1:2] * velocity
    own_cols = guided.shape[1] // lax.axis_size("cfg")
    col_start = lax.axis_index("cfg") * own_cols
    velocity_part = lax.dynamic_slice_in_dim(velocity, col_start, own_cols, 1)
    latent_part = lax.dynamic_slice_in_dim(new_latent, col_start, own_cols, 1)
    return (latent_part, velocity_part, factor * peak_speed)


def solution(mesh):
    in_specs = (
        P(("req", "tp"), None),
        P("cfg", ("req", "tp"), None),
        P(),
        P("cfg", None),
        P(),
        P(),
        P(None, None, "tp"),
        P("tp", None),
        P(None, "tp"),
        P(None, "tp"),
        P("tp", None),
        P(),
        P("cfg", None, None, None, "tp"),
        P(("cfg", "tp"), None),
        P(("cfg", "tp"), None),
        P(),
    )
    out_specs = (P(("req", "tp"), "cfg"), P(("req", "tp"), "cfg"), P())
    return jax.shard_map(shards, mesh=mesh, in_specs=in_specs, out_specs=out_specs, check_vma=False)
```

```python
import jax
import jax.numpy as jnp
from jax import lax
from jax.sharding import PartitionSpec as P

HEADS = 12
HD = 128
STEPS = 50


key_block = 1024
guide_scale = 5.0
rescale_mix = 0.7
flow_shift = 5.0
norm_eps = 1e-06
stat_eps = 1e-05


def swapped(value, axis, stride):
    mask = 2**stride
    pairs = [(source, source ^ mask) for source in range(lax.axis_size(axis))]
    return lax.ppermute(value, axis, pairs)


def shifted(value, axis, step):
    size = lax.axis_size(axis)
    return lax.ppermute(value, axis, [(source, (source + step) % size) for source in range(size)])


def ring_gather(value, axis):
    size = lax.axis_size(axis)
    forward, backward = value, value
    ahead, behind = [], []
    for unused in range(size // 2):
        forward = shifted(forward, axis, 1)
        behind.append(forward)
    for unused in range((size - 1) // 2):
        backward = shifted(backward, axis, -1)
        ahead.append(backward)
    by_offset = jnp.stack([value] + ahead + behind[::-1])
    doubled = jnp.concatenate([by_offset, by_offset], axis=0)
    start = (size - lax.axis_index(axis)) % size
    ordered = lax.dynamic_slice_in_dim(doubled, start, size, axis=0)
    return ordered.reshape((size * value.shape[0],) + value.shape[1:])


def scatter_sum(value, axis):
    size = lax.axis_size(axis)
    me = lax.axis_index(axis)
    blocks = value.reshape((size, value.shape[0] // size) + value.shape[1:])
    total = lax.dynamic_index_in_dim(blocks, me, 0, keepdims=False).astype(jnp.float32)
    for step in range(1, size):
        outgoing = lax.dynamic_index_in_dim(blocks, (me + step) % size, 0, keepdims=False)
        total = total + shifted(outgoing, axis, step).astype(jnp.float32)
    return total


def butterfly_sum(value, axis):
    stride = 1
    while stride < lax.axis_size(axis):
        value = value + swapped(value, axis, stride.bit_length() - 1)
        stride *= 2
    return value


def layer_norm(values):
    average = jnp.mean(values, axis=-1, keepdims=True)
    centered = values - average
    spread = jnp.mean(centered * centered, axis=-1, keepdims=True)
    return centered * lax.rsqrt(spread + norm_eps)


def rms_scale(values, square_sum, width, gains):
    return (values * lax.rsqrt(square_sum / width + norm_eps)[:, None] * gains).astype(jnp.bfloat16)


def request_of(positions, request_ends):
    return jnp.sum((positions[:, None] >= request_ends[None, :]).astype(jnp.int32), axis=1)


def presence(request_ids, request_count):
    return jnp.any(
        request_ids[:, None] == jnp.arange(request_count, dtype=jnp.int32)[None, :], axis=0
    )


def attend(running, queries, query_req, key_rows, value_rows, key_req, head_count, head_width):
    numerator, denominator = running
    query_count = queries.shape[0]
    key_count = key_rows.shape[0]
    scores = jnp.einsum(
        "qhd,khd->hqk",
        queries.reshape(query_count, head_count, head_width),
        key_rows.reshape(key_count, head_count, head_width),
        preferred_element_type=jnp.float32,
    ) * head_width ** (-0.5)
    same_req = query_req[:, None] == key_req[None, :]
    weights = jnp.where(same_req[None, :, :], jnp.exp(scores), 0.0)
    partial_sum = jnp.einsum(
        "hqk,khd->qhd",
        weights.astype(jnp.bfloat16),
        value_rows.reshape(key_count, head_count, head_width),
        preferred_element_type=jnp.float32,
    )
    return (
        numerator + partial_sum.reshape(query_count, head_count * head_width),
        denominator + jnp.transpose(jnp.sum(weights, axis=2)),
    )


def finish_heads(running, keep_cols, head_count, head_width):
    numerator, denominator = running
    query_count = numerator.shape[0]
    mixed = numerator.reshape(query_count, head_count, head_width) / denominator[:, :, None]
    return (mixed.reshape(query_count, head_count * head_width) * keep_cols).astype(jnp.bfloat16)


def fold_keys(
    running,
    queries,
    query_req,
    key_rows,
    value_rows,
    request_ends,
    all_tokens,
    head_count,
    head_width,
):
    key_total = key_rows.shape[0]
    request_count = request_ends.shape[0]
    wanted = presence(query_req, request_count)

    def visit_block(current, key_part, value_part, part_start):
        part_rows = key_part.shape[0]
        key_pos = part_start + jnp.arange(part_rows, dtype=jnp.int32)
        inside = (key_pos >= 0) & (key_pos < all_tokens)
        key_req = jnp.where(inside, request_of(key_pos, request_ends), -1)
        intersection = jnp.any(wanted & presence(key_req, request_count))

        def compute(state_now):
            return attend(
                state_now, queries, query_req, key_part, value_part, key_req, head_count, head_width
            )

        def skip(state_now):
            return state_now

        return lax.cond(intersection, compute, skip, current)

    full_blocks = key_total // key_block
    for index in range(full_blocks):
        lower = index * key_block
        running = visit_block(
            running,
            key_rows[lower : lower + key_block],
            value_rows[lower : lower + key_block],
            lower,
        )
    return running


def gather_project(row_block, weight):
    return jnp.dot(ring_gather(row_block, "tp"), weight, preferred_element_type=jnp.float32)


def scatter_project(mixed, weight):
    return scatter_sum(
        jnp.dot(mixed, weight, preferred_element_type=jnp.float32).astype(jnp.bfloat16), "tp"
    )


def feed_forward(ffn_rows, in_weight, out_weight):
    partner_in, partner_out = swapped((in_weight, out_weight), "cfg", 0)
    units = in_weight.shape[0]
    rows = ring_gather(ffn_rows, "tp")
    up_part = lax.dot_general(
        rows,
        jnp.concatenate([in_weight, partner_in], axis=0),
        (((1,), (1,)), ((), ())),
        preferred_element_type=jnp.float32,
    )
    activated = jax.nn.gelu(up_part, approximate=True).astype(jnp.bfloat16)
    own_term = jnp.dot(activated[:, :units], out_weight, preferred_element_type=jnp.float32)
    partner_term = jnp.dot(activated[:, units:], partner_out, preferred_element_type=jnp.float32)
    pair = own_term.astype(jnp.bfloat16).astype(jnp.float32) + partner_term.astype(
        jnp.bfloat16
    ).astype(jnp.float32)
    return scatter_sum(pair.astype(jnp.bfloat16), "tp")


def noise_level(step_value):
    fraction = 1.0 - step_value / STEPS
    return flow_shift * fraction / (1.0 + (flow_shift - 1.0) * fraction)


def shards(
    latent,
    states,
    token_counts,
    text_lens,
    steps_index,
    modulation,
    self_qkv,
    self_out,
    qk_gains,
    cross_query,
    cross_out,
    cross_gain,
    text_kv,
    ffn_in_weight,
    ffn_out_weight,
    head_weight,
):
    row_count = latent.shape[0]
    head_width = HD
    local_cols = self_out.shape[0]
    head_count = local_cols // head_width
    model_width = head_weight.shape[0]
    request_count = token_counts.shape[0]
    tp_parts = lax.axis_size("tp")
    block_rows = row_count * tp_parts
    all_tokens = block_rows * lax.axis_size("req")
    request_ends = jnp.cumsum(token_counts)
    request_range = jnp.arange(request_count, dtype=jnp.int32)
    row_pos = (lax.axis_index("req") * tp_parts + lax.axis_index("tp")) * row_count + jnp.arange(
        row_count, dtype=jnp.int32
    )
    row_onehot = (request_of(row_pos, request_ends)[:, None] == request_range[None, :]).astype(
        jnp.float32
    )
    block_first = lax.axis_index("req") * block_rows
    query_req = request_of(block_first + jnp.arange(block_rows, dtype=jnp.int32), request_ends)
    head_ids = lax.axis_index("tp") * head_count + jnp.arange(head_count, dtype=jnp.int32)
    keep_cols = jnp.repeat((head_ids < HEADS).astype(jnp.float32), head_width)
    hidden_zero = states[0]
    text_local = text_kv[0]
    text_slots = text_local.shape[2]
    text_raw = (
        text_local[:, 0].reshape(request_count * text_slots, local_cols).astype(jnp.float32)
        * keep_cols
    )
    row_mods = jnp.dot(
        row_onehot,
        modulation.reshape(request_count, 6 * model_width),
        precision=lax.Precision.HIGHEST,
    )
    shift_attn = row_mods[:, :model_width]
    scale_attn = row_mods[:, model_width : 2 * model_width]
    gate_attn = row_mods[:, 2 * model_width : 3 * model_width]
    shift_ffn = row_mods[:, 3 * model_width : 4 * model_width]
    scale_ffn = row_mods[:, 4 * model_width : 5 * model_width]
    gate_ffn = row_mods[:, 5 * model_width :]
    normed = (layer_norm(hidden_zero) * (1.0 + scale_attn) + shift_attn).astype(jnp.bfloat16)
    projected = gather_project(normed, self_qkv.reshape(model_width, 3 * local_cols))
    query_raw = projected[:, :local_cols] * keep_cols
    key_raw = projected[:, local_cols : 2 * local_cols] * keep_cols
    norm_sums = butterfly_sum(
        jnp.concatenate(
            [
                jnp.sum(query_raw * query_raw, axis=1),
                jnp.sum(key_raw * key_raw, axis=1),
                jnp.sum(text_raw * text_raw, axis=1),
            ]
        ),
        "tp",
    )
    query_sq = norm_sums[:block_rows]
    key_sq = norm_sums[block_rows : 2 * block_rows]
    text_sq = norm_sums[2 * block_rows :]
    queries = rms_scale(query_raw, query_sq, model_width, qk_gains[0])
    key_rows = rms_scale(key_raw, key_sq, model_width, qk_gains[1])
    value_rows = projected[:, 2 * local_cols :].astype(jnp.bfloat16)
    kv_all = lax.all_gather(jnp.stack([key_rows, value_rows]), "req", axis=1, tiled=True)
    key_all = kv_all[0]
    value_all = kv_all[1]
    start_state = (
        jnp.zeros((block_rows, local_cols), jnp.float32),
        jnp.zeros((block_rows, head_count), jnp.float32),
    )
    running = fold_keys(
        start_state,
        queries,
        query_req,
        key_all,
        value_all,
        request_ends,
        all_tokens,
        head_count,
        head_width,
    )
    self_mix = finish_heads(running, keep_cols, head_count, head_width)
    hidden_one = hidden_zero + gate_attn * scatter_project(self_mix, self_out)
    cross_in = (layer_norm(hidden_one) * cross_gain).astype(jnp.bfloat16)
    cross_raw = gather_project(cross_in, cross_query) * keep_cols
    cross_sq = butterfly_sum(jnp.sum(cross_raw * cross_raw, axis=1), "tp")
    cross_q = rms_scale(cross_raw, cross_sq, model_width, qk_gains[2])
    text_keys = rms_scale(text_raw, text_sq, model_width, qk_gains[3])
    text_values = text_local[:, 1].reshape(request_count * text_slots, local_cols)
    text_req = jnp.repeat(request_range, text_slots)
    text_pos = jnp.tile(jnp.arange(text_slots, dtype=jnp.int32), request_count)
    text_limit = jnp.sum(
        jnp.where(text_req[:, None] == request_range[None, :], text_lens[0][None, :], 0), axis=1
    )
    text_req = jnp.where(text_pos < text_limit, text_req, -1)
    cross_state = attend(
        start_state, cross_q, query_req, text_keys, text_values, text_req, head_count, head_width
    )
    cross_mix = finish_heads(cross_state, keep_cols, head_count, head_width)
    hidden_two = hidden_one + scatter_project(cross_mix, cross_out)
    ffn_in = (layer_norm(hidden_two) * (1.0 + scale_ffn) + shift_ffn).astype(jnp.bfloat16)
    hidden_three = hidden_two + gate_ffn * feed_forward(ffn_in, ffn_in_weight, ffn_out_weight)
    velocity_own = jnp.dot(
        layer_norm(hidden_three).astype(jnp.bfloat16),
        head_weight,
        preferred_element_type=jnp.float32,
    )
    velocity_other = swapped(velocity_own, "cfg", 0)
    first_half = lax.axis_index("cfg") == 0
    cond_speed = jnp.where(first_half, velocity_own, velocity_other)
    plain_speed = jnp.where(first_half, velocity_other, velocity_own)
    guided = plain_speed + guide_scale * (cond_speed - plain_speed)
    row_squares = jnp.stack(
        [jnp.sum(cond_speed * cond_speed, axis=1), jnp.sum(guided * guided, axis=1)], axis=1
    )
    square_sums = jnp.dot(jnp.transpose(row_onehot), row_squares, precision=lax.Precision.HIGHEST)
    peak_speed = jnp.max(row_onehot * jnp.max(jnp.abs(guided), axis=1)[:, None], axis=0)
    packed = jnp.concatenate([square_sums.reshape(-1), peak_speed])
    sum_count = 2 * request_count
    for axis in ("tp", "req"):
        stride = 1
        while stride < lax.axis_size(axis):
            other = swapped(packed, axis, stride.bit_length() - 1)
            packed = jnp.concatenate(
                [packed[:sum_count] + other[:sum_count], jnp.maximum(packed[sum_count:], other[sum_count:])]
            )
            stride *= 2
    square_sums = packed[:sum_count].reshape(request_count, 2)
    peak_speed = packed[sum_count:]
    entry_counts = token_counts.astype(jnp.float32) * guided.shape[1]
    cond_rms = jnp.sqrt(square_sums[:, 0] / entry_counts + stat_eps)
    guided_rms = jnp.sqrt(square_sums[:, 1] / entry_counts + stat_eps)
    factor = rescale_mix * cond_rms / guided_rms + (1.0 - rescale_mix)
    step_value = steps_index.astype(jnp.float32)
    delta_t = noise_level(step_value + 1.0) - noise_level(step_value)
    per_row = jnp.dot(
        row_onehot, jnp.stack([factor, delta_t], axis=1), precision=lax.Precision.HIGHEST
    )
    velocity = per_row[:, 0:1] * guided
    new_latent = latent + per_row[:, 1:2] * velocity
    own_cols = guided.shape[1] // lax.axis_size("cfg")
    col_start = lax.axis_index("cfg") * own_cols
    velocity_part = lax.dynamic_slice_in_dim(velocity, col_start, own_cols, 1)
    latent_part = lax.dynamic_slice_in_dim(new_latent, col_start, own_cols, 1)
    return (latent_part, velocity_part, factor * peak_speed)


def solution(mesh):
    in_specs = (
        P(("req", "tp"), None),
        P("cfg", ("req", "tp"), None),
        P(),
        P("cfg", None),
        P(),
        P(),
        P(None, None, "tp"),
        P("tp", None),
        P(None, "tp"),
        P(None, "tp"),
        P("tp", None),
        P(),
        P("cfg", None, None, None, "tp"),
        P(("cfg", "tp"), None),
        P(("cfg", "tp"), None),
        P(),
    )
    out_specs = (P(("req", "tp"), "cfg"), P(("req", "tp"), "cfg"), P())
    return jax.shard_map(shards, mesh=mesh, in_specs=in_specs, out_specs=out_specs, check_vma=False)
```

```python
import jax
import jax.numpy as jnp
import functools
from jax import lax
from jax.experimental import pallas as pl
from jax.sharding import PartitionSpec as P

HEADS = 12
HD = 128
STEPS = 50


key_block = 1024
guide_scale = 5.0
rescale_mix = 0.7
flow_shift = 5.0
norm_eps = 1e-06
stat_eps = 1e-05


def swapped(value, axis, stride):
    mask = 2**stride
    pairs = [(source, source ^ mask) for source in range(lax.axis_size(axis))]
    return lax.ppermute(value, axis, pairs)


def shifted(value, axis, step):
    size = lax.axis_size(axis)
    return lax.ppermute(value, axis, [(source, (source + step) % size) for source in range(size)])


def ring_gather(value, axis):
    size = lax.axis_size(axis)
    forward, backward = value, value
    ahead, behind = [], []
    for unused in range(size // 2):
        forward = shifted(forward, axis, 1)
        behind.append(forward)
    for unused in range((size - 1) // 2):
        backward = shifted(backward, axis, -1)
        ahead.append(backward)
    by_offset = jnp.stack([value] + ahead + behind[::-1])
    doubled = jnp.concatenate([by_offset, by_offset], axis=0)
    start = (size - lax.axis_index(axis)) % size
    ordered = lax.dynamic_slice_in_dim(doubled, start, size, axis=0)
    return ordered.reshape((size * value.shape[0],) + value.shape[1:])


def scatter_sum(value, axis):
    size = lax.axis_size(axis)
    me = lax.axis_index(axis)
    blocks = value.reshape((size, value.shape[0] // size) + value.shape[1:])
    total = lax.dynamic_index_in_dim(blocks, me, 0, keepdims=False).astype(jnp.float32)
    for step in range(1, size):
        outgoing = lax.dynamic_index_in_dim(blocks, (me + step) % size, 0, keepdims=False)
        total = total + shifted(outgoing, axis, step).astype(jnp.float32)
    return total


def butterfly_sum(value, axis):
    stride = 1
    while stride < lax.axis_size(axis):
        value = value + swapped(value, axis, stride.bit_length() - 1)
        stride *= 2
    return value


def layer_norm(values):
    average = jnp.mean(values, axis=-1, keepdims=True)
    centered = values - average
    spread = jnp.mean(centered * centered, axis=-1, keepdims=True)
    return centered * lax.rsqrt(spread + norm_eps)


def rms_scale(values, square_sum, width, gains):
    return (values * lax.rsqrt(square_sum / width + norm_eps)[:, None] * gains).astype(jnp.bfloat16)


def request_of(positions, request_ends):
    return jnp.sum((positions[:, None] >= request_ends[None, :]).astype(jnp.int32), axis=1)


def attention_body(head_count, head_width, q_ref, k_ref, v_ref, qreq_ref, kreq_ref, num_ref, den_ref):
    @pl.when(pl.program_id(0) == 0)
    def _():
        num_ref[...] = jnp.zeros_like(num_ref)
        den_ref[...] = jnp.zeros_like(den_ref)

    same_req = qreq_ref[...] == kreq_ref[...]
    for head in range(head_count):
        cols = slice(head * head_width, (head + 1) * head_width)
        scores = lax.dot_general(
            q_ref[:, cols], k_ref[:, cols], (((1,), (1,)), ((), ())), preferred_element_type=jnp.float32
        ) * head_width ** (-0.5)
        weights = jnp.where(same_req, jnp.exp(scores), 0.0)
        num_ref[:, cols] += jnp.dot(
            weights.astype(jnp.bfloat16), v_ref[:, cols], preferred_element_type=jnp.float32
        )
        den_ref[:, cols] += jnp.broadcast_to(jnp.sum(weights, axis=1, keepdims=True), (weights.shape[0], head_width))


def attention_sums(queries, query_req, key_rows, value_rows, key_req, head_count, head_width, key_block):
    query_count, width = queries.shape
    key_count = key_rows.shape[0]
    steps = key_count // key_block
    flops = 4 * query_count * key_count * width
    return pl.pallas_call(
        functools.partial(attention_body, head_count, head_width),
        grid=(steps,),
        in_specs=[
            pl.BlockSpec((query_count, width), lambda j: (0, 0)),
            pl.BlockSpec((key_block, width), lambda j: (j, 0)),
            pl.BlockSpec((key_block, width), lambda j: (j, 0)),
            pl.BlockSpec((query_count, 1), lambda j: (0, 0)),
            pl.BlockSpec((1, key_block), lambda j: (0, j)),
        ],
        out_specs=[
            pl.BlockSpec((query_count, width), lambda j: (0, 0)),
            pl.BlockSpec((query_count, width), lambda j: (0, 0)),
        ],
        out_shape=[
            jax.ShapeDtypeStruct((query_count, width), jnp.float32),
            jax.ShapeDtypeStruct((query_count, width), jnp.float32),
        ],
        cost_estimate=pl.CostEstimate(
            flops=flops,
            transcendentals=query_count * key_count * head_count,
            bytes_accessed=2 * (query_count + 2 * key_count) * width + 8 * query_count * width,
        ),
    )(queries, key_rows, value_rows, query_req.reshape(query_count, 1), key_req.reshape(1, key_count))


def gather_project(row_block, weight):
    return jnp.dot(ring_gather(row_block, "tp"), weight, preferred_element_type=jnp.float32)


def scatter_project(mixed, weight):
    return scatter_sum(
        jnp.dot(mixed, weight, preferred_element_type=jnp.float32).astype(jnp.bfloat16), "tp"
    )


def feed_forward(ffn_rows, in_weight, out_weight):
    partner_in, partner_out = swapped((in_weight, out_weight), "cfg", 0)
    units = in_weight.shape[0]
    rows = ring_gather(ffn_rows, "tp")
    up_part = lax.dot_general(
        rows,
        jnp.concatenate([in_weight, partner_in], axis=0),
        (((1,), (1,)), ((), ())),
        preferred_element_type=jnp.float32,
    )
    activated = jax.nn.gelu(up_part, approximate=True).astype(jnp.bfloat16)
    own_term = jnp.dot(activated[:, :units], out_weight, preferred_element_type=jnp.float32)
    partner_term = jnp.dot(activated[:, units:], partner_out, preferred_element_type=jnp.float32)
    pair = own_term.astype(jnp.bfloat16).astype(jnp.float32) + partner_term.astype(
        jnp.bfloat16
    ).astype(jnp.float32)
    return scatter_sum(pair.astype(jnp.bfloat16), "tp")


def noise_level(step_value):
    fraction = 1.0 - step_value / STEPS
    return flow_shift * fraction / (1.0 + (flow_shift - 1.0) * fraction)


def shards(
    latent,
    states,
    token_counts,
    text_lens,
    steps_index,
    modulation,
    self_qkv,
    self_out,
    qk_gains,
    cross_query,
    cross_out,
    cross_gain,
    text_kv,
    ffn_in_weight,
    ffn_out_weight,
    head_weight,
):
    row_count = latent.shape[0]
    head_width = HD
    local_cols = self_out.shape[0]
    head_count = local_cols // head_width
    model_width = head_weight.shape[0]
    request_count = token_counts.shape[0]
    tp_parts = lax.axis_size("tp")
    block_rows = row_count * tp_parts
    all_tokens = block_rows * lax.axis_size("req")
    request_ends = jnp.cumsum(token_counts)
    request_range = jnp.arange(request_count, dtype=jnp.int32)
    row_pos = (lax.axis_index("req") * tp_parts + lax.axis_index("tp")) * row_count + jnp.arange(
        row_count, dtype=jnp.int32
    )
    row_onehot = (request_of(row_pos, request_ends)[:, None] == request_range[None, :]).astype(
        jnp.float32
    )
    block_first = lax.axis_index("req") * block_rows
    query_req = request_of(block_first + jnp.arange(block_rows, dtype=jnp.int32), request_ends)
    head_ids = lax.axis_index("tp") * head_count + jnp.arange(head_count, dtype=jnp.int32)
    keep_cols = jnp.repeat((head_ids < HEADS).astype(jnp.float32), head_width)
    hidden_zero = states[0]
    text_local = text_kv[0]
    text_slots = text_local.shape[2]
    text_raw = (
        text_local[:, 0].reshape(request_count * text_slots, local_cols).astype(jnp.float32)
        * keep_cols
    )
    row_mods = jnp.dot(
        row_onehot,
        modulation.reshape(request_count, 6 * model_width),
        precision=lax.Precision.HIGHEST,
    )
    shift_attn = row_mods[:, :model_width]
    scale_attn = row_mods[:, model_width : 2 * model_width]
    gate_attn = row_mods[:, 2 * model_width : 3 * model_width]
    shift_ffn = row_mods[:, 3 * model_width : 4 * model_width]
    scale_ffn = row_mods[:, 4 * model_width : 5 * model_width]
    gate_ffn = row_mods[:, 5 * model_width :]
    normed = (layer_norm(hidden_zero) * (1.0 + scale_attn) + shift_attn).astype(jnp.bfloat16)
    projected = gather_project(normed, self_qkv.reshape(model_width, 3 * local_cols))
    query_raw = projected[:, :local_cols] * keep_cols
    key_raw = projected[:, local_cols : 2 * local_cols] * keep_cols
    norm_sums = butterfly_sum(
        jnp.concatenate(
            [
                jnp.sum(query_raw * query_raw, axis=1),
                jnp.sum(key_raw * key_raw, axis=1),
                jnp.sum(text_raw * text_raw, axis=1),
            ]
        ),
        "tp",
    )
    query_sq = norm_sums[:block_rows]
    key_sq = norm_sums[block_rows : 2 * block_rows]
    text_sq = norm_sums[2 * block_rows :]
    queries = rms_scale(query_raw, query_sq, model_width, qk_gains[0])
    key_rows = rms_scale(key_raw, key_sq, model_width, qk_gains[1])
    value_rows = projected[:, 2 * local_cols :].astype(jnp.bfloat16)
    kv_all = lax.all_gather(jnp.stack([key_rows, value_rows]), "req", axis=1, tiled=True)
    key_all = kv_all[0]
    value_all = kv_all[1]
    key_pos = jnp.arange(all_tokens, dtype=jnp.int32)
    self_num, self_den = attention_sums(
        queries,
        query_req,
        key_all,
        value_all,
        request_of(key_pos, request_ends),
        head_count,
        head_width,
        key_block,
    )
    self_mix = (self_num / self_den * keep_cols).astype(jnp.bfloat16)
    hidden_one = hidden_zero + gate_attn * scatter_project(self_mix, self_out)
    cross_in = (layer_norm(hidden_one) * cross_gain).astype(jnp.bfloat16)
    cross_raw = gather_project(cross_in, cross_query) * keep_cols
    cross_sq = butterfly_sum(jnp.sum(cross_raw * cross_raw, axis=1), "tp")
    cross_q = rms_scale(cross_raw, cross_sq, model_width, qk_gains[2])
    text_keys = rms_scale(text_raw, text_sq, model_width, qk_gains[3])
    text_values = text_local[:, 1].reshape(request_count * text_slots, local_cols)
    text_req = jnp.repeat(request_range, text_slots)
    text_pos = jnp.tile(jnp.arange(text_slots, dtype=jnp.int32), request_count)
    text_limit = jnp.sum(
        jnp.where(text_req[:, None] == request_range[None, :], text_lens[0][None, :], 0), axis=1
    )
    text_req = jnp.where(text_pos < text_limit, text_req, -1)
    cross_num, cross_den = attention_sums(
        cross_q, query_req, text_keys, text_values, text_req, head_count, head_width, text_slots
    )
    cross_mix = (cross_num / cross_den * keep_cols).astype(jnp.bfloat16)
    hidden_two = hidden_one + scatter_project(cross_mix, cross_out)
    ffn_in = (layer_norm(hidden_two) * (1.0 + scale_ffn) + shift_ffn).astype(jnp.bfloat16)
    hidden_three = hidden_two + gate_ffn * feed_forward(ffn_in, ffn_in_weight, ffn_out_weight)
    velocity_own = jnp.dot(
        layer_norm(hidden_three).astype(jnp.bfloat16),
        head_weight,
        preferred_element_type=jnp.float32,
    )
    velocity_other = swapped(velocity_own, "cfg", 0)
    first_half = lax.axis_index("cfg") == 0
    cond_speed = jnp.where(first_half, velocity_own, velocity_other)
    plain_speed = jnp.where(first_half, velocity_other, velocity_own)
    guided = plain_speed + guide_scale * (cond_speed - plain_speed)
    row_squares = jnp.stack(
        [jnp.sum(cond_speed * cond_speed, axis=1), jnp.sum(guided * guided, axis=1)], axis=1
    )
    square_sums = jnp.dot(jnp.transpose(row_onehot), row_squares, precision=lax.Precision.HIGHEST)
    peak_speed = jnp.max(row_onehot * jnp.max(jnp.abs(guided), axis=1)[:, None], axis=0)
    packed = jnp.concatenate([square_sums.reshape(-1), peak_speed])
    sum_count = 2 * request_count
    for axis in ("tp", "req"):
        stride = 1
        while stride < lax.axis_size(axis):
            other = swapped(packed, axis, stride.bit_length() - 1)
            packed = jnp.concatenate(
                [packed[:sum_count] + other[:sum_count], jnp.maximum(packed[sum_count:], other[sum_count:])]
            )
            stride *= 2
    square_sums = packed[:sum_count].reshape(request_count, 2)
    peak_speed = packed[sum_count:]
    entry_counts = token_counts.astype(jnp.float32) * guided.shape[1]
    cond_rms = jnp.sqrt(square_sums[:, 0] / entry_counts + stat_eps)
    guided_rms = jnp.sqrt(square_sums[:, 1] / entry_counts + stat_eps)
    factor = rescale_mix * cond_rms / guided_rms + (1.0 - rescale_mix)
    step_value = steps_index.astype(jnp.float32)
    delta_t = noise_level(step_value + 1.0) - noise_level(step_value)
    per_row = jnp.dot(
        row_onehot, jnp.stack([factor, delta_t], axis=1), precision=lax.Precision.HIGHEST
    )
    velocity = per_row[:, 0:1] * guided
    new_latent = latent + per_row[:, 1:2] * velocity
    own_cols = guided.shape[1] // lax.axis_size("cfg")
    col_start = lax.axis_index("cfg") * own_cols
    velocity_part = lax.dynamic_slice_in_dim(velocity, col_start, own_cols, 1)
    latent_part = lax.dynamic_slice_in_dim(new_latent, col_start, own_cols, 1)
    return (latent_part, velocity_part, factor * peak_speed)


def solution(mesh):
    in_specs = (
        P(("req", "tp"), None),
        P("cfg", ("req", "tp"), None),
        P(),
        P("cfg", None),
        P(),
        P(),
        P(None, None, "tp"),
        P("tp", None),
        P(None, "tp"),
        P(None, "tp"),
        P("tp", None),
        P(),
        P("cfg", None, None, None, "tp"),
        P(("cfg", "tp"), None),
        P(("cfg", "tp"), None),
        P(),
    )
    out_specs = (P(("req", "tp"), "cfg"), P(("req", "tp"), "cfg"), P())
    return jax.shard_map(shards, mesh=mesh, in_specs=in_specs, out_specs=out_specs, check_vma=False)
```

```python
import jax
import jax.numpy as jnp
import functools
from jax import lax
from jax.experimental import pallas as pl
from jax.sharding import PartitionSpec as P

HEADS = 12
HD = 128
STEPS = 50


key_block = 1024
guide_scale = 5.0
rescale_mix = 0.7
flow_shift = 5.0
norm_eps = 1e-06
stat_eps = 1e-05


def swapped(value, axis, stride):
    mask = 2**stride
    pairs = [(source, source ^ mask) for source in range(lax.axis_size(axis))]
    return lax.ppermute(value, axis, pairs)


def shifted(value, axis, step):
    size = lax.axis_size(axis)
    return lax.ppermute(value, axis, [(source, (source + step) % size) for source in range(size)])


def ring_gather(value, axis):
    size = lax.axis_size(axis)
    forward, backward = value, value
    ahead, behind = [], []
    for unused in range(size // 2):
        forward = shifted(forward, axis, 1)
        behind.append(forward)
    for unused in range((size - 1) // 2):
        backward = shifted(backward, axis, -1)
        ahead.append(backward)
    return jnp.concatenate([value] + ahead + behind[::-1], axis=0)


def scatter_sum(value, axis):
    size = lax.axis_size(axis)
    rows = value.shape[0] // size
    total = value[:rows].astype(jnp.float32)
    for step in range(1, size):
        outgoing = value[step * rows : (step + 1) * rows]
        total = total + shifted(outgoing, axis, step).astype(jnp.float32)
    return total


def offset_blocks(value, axis, to_natural):
    size = lax.axis_size(axis)
    me = lax.axis_index(axis)
    blocks = value.reshape(size, value.shape[0] // size)
    doubled = jnp.concatenate([blocks, blocks], axis=0)
    start = (size - me) % size if to_natural else me
    return lax.dynamic_slice_in_dim(doubled, start, size, axis=0).reshape(value.shape)


def natural_butterfly(row_values, axis):
    natural = offset_blocks(row_values, axis, True)
    return offset_blocks(butterfly_sum(natural, axis), axis, False)


def butterfly_sum(value, axis):
    stride = 1
    while stride < lax.axis_size(axis):
        value = value + swapped(value, axis, stride.bit_length() - 1)
        stride *= 2
    return value


def layer_norm(values):
    average = jnp.mean(values, axis=-1, keepdims=True)
    centered = values - average
    spread = jnp.mean(centered * centered, axis=-1, keepdims=True)
    return centered * lax.rsqrt(spread + norm_eps)


def rms_scale(values, square_sum, width, gains):
    return (values * lax.rsqrt(square_sum / width + norm_eps)[:, None] * gains).astype(jnp.bfloat16)


def request_of(positions, request_ends):
    return jnp.sum((positions[:, None] >= request_ends[None, :]).astype(jnp.int32), axis=1)


def attention_body(head_count, head_width, q_ref, k_ref, v_ref, qreq_ref, kreq_ref, num_ref, den_ref):
    @pl.when(pl.program_id(0) == 0)
    def _():
        num_ref[...] = jnp.zeros_like(num_ref)
        den_ref[...] = jnp.zeros_like(den_ref)

    same_req = qreq_ref[...] == kreq_ref[...]
    for head in range(head_count):
        cols = slice(head * head_width, (head + 1) * head_width)
        scores = lax.dot_general(
            q_ref[:, cols], k_ref[:, cols], (((1,), (1,)), ((), ())), preferred_element_type=jnp.float32
        ) * head_width ** (-0.5)
        weights = jnp.where(same_req, jnp.exp(scores), 0.0)
        num_ref[:, cols] += jnp.dot(
            weights.astype(jnp.bfloat16), v_ref[:, cols], preferred_element_type=jnp.float32
        )
        den_ref[:, cols] += jnp.broadcast_to(jnp.sum(weights, axis=1, keepdims=True), (weights.shape[0], head_width))


def attention_sums(queries, query_req, key_value, key_req, head_count, head_width, key_block):
    query_count, width = queries.shape
    key_count = key_value.shape[1]
    steps = key_count // key_block
    flops = 4 * query_count * key_count * width
    return pl.pallas_call(
        functools.partial(attention_body, head_count, head_width),
        grid=(steps,),
        in_specs=[
            pl.BlockSpec((query_count, width), lambda j: (0, 0)),
            pl.BlockSpec((None, key_block, width), lambda j: (0, j, 0)),
            pl.BlockSpec((None, key_block, width), lambda j: (1, j, 0)),
            pl.BlockSpec((query_count, 1), lambda j: (0, 0)),
            pl.BlockSpec((1, key_block), lambda j: (0, j)),
        ],
        out_specs=[
            pl.BlockSpec((query_count, width), lambda j: (0, 0)),
            pl.BlockSpec((query_count, width), lambda j: (0, 0)),
        ],
        out_shape=[
            jax.ShapeDtypeStruct((query_count, width), jnp.float32),
            jax.ShapeDtypeStruct((query_count, width), jnp.float32),
        ],
        cost_estimate=pl.CostEstimate(
            flops=flops,
            transcendentals=query_count * key_count * head_count,
            bytes_accessed=2 * (query_count + 2 * key_count) * width + 8 * query_count * width,
        ),
    )(queries, key_value, key_value, query_req.reshape(query_count, 1), key_req.reshape(1, key_count))


def gather_project(row_block, weight):
    return jnp.dot(ring_gather(row_block, "tp"), weight, preferred_element_type=jnp.float32)


def scatter_project(mixed, weight):
    return scatter_sum(
        jnp.dot(mixed, weight, preferred_element_type=jnp.float32).astype(jnp.bfloat16), "tp"
    )


def feed_forward(ffn_rows, in_weight, out_weight):
    partner_in, partner_out = swapped((in_weight, out_weight), "cfg", 0)
    units = in_weight.shape[0]
    rows = ring_gather(ffn_rows, "tp")
    up_part = lax.dot_general(
        rows,
        jnp.concatenate([in_weight, partner_in], axis=0),
        (((1,), (1,)), ((), ())),
        preferred_element_type=jnp.float32,
    )
    activated = jax.nn.gelu(up_part, approximate=True).astype(jnp.bfloat16)
    own_term = jnp.dot(activated[:, :units], out_weight, preferred_element_type=jnp.float32)
    partner_term = jnp.dot(activated[:, units:], partner_out, preferred_element_type=jnp.float32)
    pair = own_term.astype(jnp.bfloat16).astype(jnp.float32) + partner_term.astype(
        jnp.bfloat16
    ).astype(jnp.float32)
    return scatter_sum(pair.astype(jnp.bfloat16), "tp")


def noise_level(step_value):
    fraction = 1.0 - step_value / STEPS
    return flow_shift * fraction / (1.0 + (flow_shift - 1.0) * fraction)


def shards(
    latent,
    states,
    token_counts,
    text_lens,
    steps_index,
    modulation,
    self_qkv,
    self_out,
    qk_gains,
    cross_query,
    cross_out,
    cross_gain,
    text_kv,
    ffn_in_weight,
    ffn_out_weight,
    head_weight,
):
    row_count = latent.shape[0]
    head_width = HD
    local_cols = self_out.shape[0]
    head_count = local_cols // head_width
    model_width = head_weight.shape[0]
    request_count = token_counts.shape[0]
    tp_parts = lax.axis_size("tp")
    block_rows = row_count * tp_parts
    all_tokens = block_rows * lax.axis_size("req")
    request_ends = jnp.cumsum(token_counts)
    request_range = jnp.arange(request_count, dtype=jnp.int32)
    row_pos = (lax.axis_index("req") * tp_parts + lax.axis_index("tp")) * row_count + jnp.arange(
        row_count, dtype=jnp.int32
    )
    row_onehot = (request_of(row_pos, request_ends)[:, None] == request_range[None, :]).astype(
        jnp.float32
    )
    block_first = lax.axis_index("req") * block_rows
    in_block = jnp.arange(block_rows, dtype=jnp.int32)
    in_block = ((lax.axis_index("tp") + in_block // row_count) % tp_parts) * row_count + (
        in_block % row_count
    )
    query_req = request_of(block_first + in_block, request_ends)
    head_ids = lax.axis_index("tp") * head_count + jnp.arange(head_count, dtype=jnp.int32)
    keep_cols = jnp.repeat((head_ids < HEADS).astype(jnp.float32), head_width)
    hidden_zero = states[0]
    text_local = text_kv[0]
    text_slots = text_local.shape[2]
    text_raw = (
        text_local[:, 0].reshape(request_count * text_slots, local_cols).astype(jnp.float32)
        * keep_cols
    )
    row_mods = jnp.dot(
        row_onehot,
        modulation.reshape(request_count, 6 * model_width),
        precision=lax.Precision.HIGHEST,
    )
    shift_attn = row_mods[:, :model_width]
    scale_attn = row_mods[:, model_width : 2 * model_width]
    gate_attn = row_mods[:, 2 * model_width : 3 * model_width]
    shift_ffn = row_mods[:, 3 * model_width : 4 * model_width]
    scale_ffn = row_mods[:, 4 * model_width : 5 * model_width]
    gate_ffn = row_mods[:, 5 * model_width :]
    normed = (layer_norm(hidden_zero) * (1.0 + scale_attn) + shift_attn).astype(jnp.bfloat16)
    projected = gather_project(normed, self_qkv.reshape(model_width, 3 * local_cols))
    query_raw = projected[:, :local_cols] * keep_cols
    key_raw = projected[:, local_cols : 2 * local_cols] * keep_cols
    row_count_sums = 2 * block_rows
    norm_sums = butterfly_sum(
        jnp.concatenate(
            [
                offset_blocks(
                    jnp.stack(
                        [jnp.sum(query_raw * query_raw, axis=1), jnp.sum(key_raw * key_raw, axis=1)],
                        axis=1,
                    ).reshape(-1),
                    "tp",
                    True,
                ),
                jnp.sum(text_raw * text_raw, axis=1),
            ]
        ),
        "tp",
    )
    row_sums = offset_blocks(norm_sums[:row_count_sums], "tp", False).reshape(block_rows, 2)
    text_sq = norm_sums[row_count_sums:]
    query_sq = row_sums[:, 0]
    key_sq = row_sums[:, 1]
    queries = rms_scale(query_raw, query_sq, model_width, qk_gains[0])
    key_rows = rms_scale(key_raw, key_sq, model_width, qk_gains[1])
    value_rows = projected[:, 2 * local_cols :].astype(jnp.bfloat16)
    kv_all = lax.all_gather(jnp.stack([key_rows, value_rows]), "req", axis=1, tiled=True)
    key_pos = jnp.arange(all_tokens, dtype=jnp.int32)
    key_pos = (key_pos // block_rows) * block_rows + jnp.tile(in_block, lax.axis_size("req"))
    self_num, self_den = attention_sums(
        queries,
        query_req,
        kv_all,
        request_of(key_pos, request_ends),
        head_count,
        head_width,
        key_block,
    )
    self_mix = (self_num / self_den * keep_cols).astype(jnp.bfloat16)
    hidden_one = hidden_zero + gate_attn * scatter_project(self_mix, self_out)
    cross_in = (layer_norm(hidden_one) * cross_gain).astype(jnp.bfloat16)
    cross_raw = gather_project(cross_in, cross_query) * keep_cols
    cross_sq = natural_butterfly(jnp.sum(cross_raw * cross_raw, axis=1), "tp")
    cross_q = rms_scale(cross_raw, cross_sq, model_width, qk_gains[2])
    text_keys = rms_scale(text_raw, text_sq, model_width, qk_gains[3])
    text_values = text_local[:, 1].reshape(request_count * text_slots, local_cols)
    text_req = jnp.repeat(request_range, text_slots)
    text_pos = jnp.tile(jnp.arange(text_slots, dtype=jnp.int32), request_count)
    text_limit = jnp.sum(
        jnp.where(text_req[:, None] == request_range[None, :], text_lens[0][None, :], 0), axis=1
    )
    text_req = jnp.where(text_pos < text_limit, text_req, -1)
    cross_num, cross_den = attention_sums(
        cross_q,
        query_req,
        jnp.stack([text_keys, text_values]),
        text_req,
        head_count,
        head_width,
        text_slots,
    )
    cross_mix = (cross_num / cross_den * keep_cols).astype(jnp.bfloat16)
    hidden_two = hidden_one + scatter_project(cross_mix, cross_out)
    ffn_in = (layer_norm(hidden_two) * (1.0 + scale_ffn) + shift_ffn).astype(jnp.bfloat16)
    hidden_three = hidden_two + gate_ffn * feed_forward(ffn_in, ffn_in_weight, ffn_out_weight)
    velocity_own = jnp.dot(
        layer_norm(hidden_three).astype(jnp.bfloat16),
        head_weight,
        preferred_element_type=jnp.float32,
    )
    velocity_other = swapped(velocity_own, "cfg", 0)
    first_half = lax.axis_index("cfg") == 0
    cond_speed = jnp.where(first_half, velocity_own, velocity_other)
    plain_speed = jnp.where(first_half, velocity_other, velocity_own)
    guided = plain_speed + guide_scale * (cond_speed - plain_speed)
    row_squares = jnp.stack(
        [jnp.sum(cond_speed * cond_speed, axis=1), jnp.sum(guided * guided, axis=1)], axis=1
    )
    square_sums = jnp.dot(jnp.transpose(row_onehot), row_squares, precision=lax.Precision.HIGHEST)
    peak_speed = jnp.max(row_onehot * jnp.max(jnp.abs(guided), axis=1)[:, None], axis=0)
    packed = jnp.concatenate([square_sums.reshape(-1), peak_speed])
    sum_count = 2 * request_count
    for axis in ("tp", "req"):
        stride = 1
        while stride < lax.axis_size(axis):
            other = swapped(packed, axis, stride.bit_length() - 1)
            packed = jnp.concatenate(
                [packed[:sum_count] + other[:sum_count], jnp.maximum(packed[sum_count:], other[sum_count:])]
            )
            stride *= 2
    square_sums = packed[:sum_count].reshape(request_count, 2)
    peak_speed = packed[sum_count:]
    entry_counts = token_counts.astype(jnp.float32) * guided.shape[1]
    cond_rms = jnp.sqrt(square_sums[:, 0] / entry_counts + stat_eps)
    guided_rms = jnp.sqrt(square_sums[:, 1] / entry_counts + stat_eps)
    factor = rescale_mix * cond_rms / guided_rms + (1.0 - rescale_mix)
    step_value = steps_index.astype(jnp.float32)
    delta_t = noise_level(step_value + 1.0) - noise_level(step_value)
    per_row = jnp.dot(
        row_onehot, jnp.stack([factor, delta_t], axis=1), precision=lax.Precision.HIGHEST
    )
    velocity = per_row[:, 0:1] * guided
    new_latent = latent + per_row[:, 1:2] * velocity
    own_cols = guided.shape[1] // lax.axis_size("cfg")
    col_start = lax.axis_index("cfg") * own_cols
    velocity_part = lax.dynamic_slice_in_dim(velocity, col_start, own_cols, 1)
    latent_part = lax.dynamic_slice_in_dim(new_latent, col_start, own_cols, 1)
    return (latent_part, velocity_part, factor * peak_speed)


def solution(mesh):
    in_specs = (
        P(("req", "tp"), None),
        P("cfg", ("req", "tp"), None),
        P(),
        P("cfg", None),
        P(),
        P(),
        P(None, None, "tp"),
        P("tp", None),
        P(None, "tp"),
        P(None, "tp"),
        P("tp", None),
        P(),
        P("cfg", None, None, None, "tp"),
        P(("cfg", "tp"), None),
        P(("cfg", "tp"), None),
        P(),
    )
    out_specs = (P(("req", "tp"), "cfg"), P(("req", "tp"), "cfg"), P())
    return jax.shard_map(shards, mesh=mesh, in_specs=in_specs, out_specs=out_specs, check_vma=False)
```

```python
import jax
import jax.numpy as jnp
import functools
from jax import lax
from jax.experimental import pallas as pl
from jax.sharding import PartitionSpec as P

HEADS = 12
HD = 128
STEPS = 50


key_block = 1024
guide_scale = 5.0
rescale_mix = 0.7
flow_shift = 5.0
norm_eps = 1e-06
stat_eps = 1e-05


def swapped(value, axis, stride):
    mask = 2**stride
    pairs = [(source, source ^ mask) for source in range(lax.axis_size(axis))]
    return lax.ppermute(value, axis, pairs)


def shifted(value, axis, step):
    size = lax.axis_size(axis)
    return lax.ppermute(value, axis, [(source, (source + step) % size) for source in range(size)])


def ring_gather(value, axis):
    size = lax.axis_size(axis)
    forward, backward = value, value
    ahead, behind = [], []
    for unused in range(size // 2):
        forward = shifted(forward, axis, 1)
        behind.append(forward)
    for unused in range((size - 1) // 2):
        backward = shifted(backward, axis, -1)
        ahead.append(backward)
    return jnp.concatenate([value] + ahead + behind[::-1], axis=0)


def scatter_sum(value, axis):
    size = lax.axis_size(axis)
    rows = value.shape[0] // size
    total = value[:rows].astype(jnp.float32)
    for step in range(1, size):
        outgoing = value[step * rows : (step + 1) * rows]
        total = total + shifted(outgoing, axis, step).astype(jnp.float32)
    return total


def offset_blocks(value, axis, to_natural):
    size = lax.axis_size(axis)
    me = lax.axis_index(axis)
    blocks = value.reshape(size, value.shape[0] // size)
    doubled = jnp.concatenate([blocks, blocks], axis=0)
    start = (size - me) % size if to_natural else me
    return lax.dynamic_slice_in_dim(doubled, start, size, axis=0).reshape(value.shape)


def natural_butterfly(row_values, axis):
    natural = offset_blocks(row_values, axis, True)
    return offset_blocks(butterfly_sum(natural, axis), axis, False)


def group_exchange(value, axis, stride, width):
    size = lax.axis_size(axis)
    own = (lax.axis_index(axis) // stride) % width
    received = [value]
    for mate in range(1, width):
        pairs = [(source, source ^ (mate * stride)) for source in range(size)]
        received.append(lax.ppermute(value, axis, pairs))
    stacked = jnp.stack(received)
    by_slot = jnp.take(stacked, jnp.arange(width, dtype=jnp.int32) ^ own, axis=0)
    return [by_slot[slot] for slot in range(width)]


def reduction_rounds(axis):
    size = lax.axis_size(axis)
    stride, rounds = 1, []
    while stride < size:
        width = 4 if size // stride >= 4 else 2
        rounds.append((stride, width))
        stride *= width
    return rounds


def butterfly_sum(value, axis):
    for stride, width in reduction_rounds(axis):
        parts = group_exchange(value, axis, stride, width)
        value = parts[0]
        for part in parts[1:]:
            value = value + part
    return value


def layer_norm(values):
    average = jnp.mean(values, axis=-1, keepdims=True)
    centered = values - average
    spread = jnp.mean(centered * centered, axis=-1, keepdims=True)
    return centered * lax.rsqrt(spread + norm_eps)


def rms_scale(values, square_sum, width, gains):
    return (values * lax.rsqrt(square_sum / width + norm_eps)[:, None] * gains).astype(jnp.bfloat16)


def request_of(positions, request_ends):
    return jnp.sum((positions[:, None] >= request_ends[None, :]).astype(jnp.int32), axis=1)


def attention_body(head_count, head_width, q_ref, k_ref, v_ref, qreq_ref, kreq_ref, num_ref, den_ref):
    @pl.when(pl.program_id(0) == 0)
    def _():
        num_ref[...] = jnp.zeros_like(num_ref)
        den_ref[...] = jnp.zeros_like(den_ref)

    same_req = qreq_ref[...] == kreq_ref[...]
    for head in range(head_count):
        cols = slice(head * head_width, (head + 1) * head_width)
        scores = lax.dot_general(
            q_ref[:, cols], k_ref[:, cols], (((1,), (1,)), ((), ())), preferred_element_type=jnp.float32
        ) * head_width ** (-0.5)
        weights = jnp.where(same_req, jnp.exp(scores), 0.0)
        num_ref[:, cols] += jnp.dot(
            weights.astype(jnp.bfloat16), v_ref[:, cols], preferred_element_type=jnp.float32
        )
        den_ref[:, cols] += jnp.broadcast_to(jnp.sum(weights, axis=1, keepdims=True), (weights.shape[0], head_width))


def attention_sums(queries, query_req, key_value, key_req, head_count, head_width, key_block):
    query_count, width = queries.shape
    key_count = key_value.shape[1]
    steps = key_count // key_block
    flops = 4 * query_count * key_count * width
    return pl.pallas_call(
        functools.partial(attention_body, head_count, head_width),
        grid=(steps,),
        in_specs=[
            pl.BlockSpec((query_count, width), lambda j: (0, 0)),
            pl.BlockSpec((None, key_block, width), lambda j: (0, j, 0)),
            pl.BlockSpec((None, key_block, width), lambda j: (1, j, 0)),
            pl.BlockSpec((query_count, 1), lambda j: (0, 0)),
            pl.BlockSpec((1, key_block), lambda j: (0, j)),
        ],
        out_specs=[
            pl.BlockSpec((query_count, width), lambda j: (0, 0)),
            pl.BlockSpec((query_count, width), lambda j: (0, 0)),
        ],
        out_shape=[
            jax.ShapeDtypeStruct((query_count, width), jnp.float32),
            jax.ShapeDtypeStruct((query_count, width), jnp.float32),
        ],
        cost_estimate=pl.CostEstimate(
            flops=flops,
            transcendentals=query_count * key_count * head_count,
            bytes_accessed=2 * (query_count + 2 * key_count) * width + 8 * query_count * width,
        ),
    )(queries, key_value, key_value, query_req.reshape(query_count, 1), key_req.reshape(1, key_count))


def gather_project(row_block, weight):
    return jnp.dot(ring_gather(row_block, "tp"), weight, preferred_element_type=jnp.float32)


def scatter_project(mixed, weight):
    return scatter_sum(
        jnp.dot(mixed, weight, preferred_element_type=jnp.float32).astype(jnp.bfloat16), "tp"
    )


def feed_forward(ffn_rows, in_weight, out_weight):
    partner_in, partner_out = swapped((in_weight, out_weight), "cfg", 0)
    units = in_weight.shape[0]
    rows = ring_gather(ffn_rows, "tp")
    up_part = lax.dot_general(
        rows,
        jnp.concatenate([in_weight, partner_in], axis=0),
        (((1,), (1,)), ((), ())),
        preferred_element_type=jnp.float32,
    )
    activated = jax.nn.gelu(up_part, approximate=True).astype(jnp.bfloat16)
    own_term = jnp.dot(activated[:, :units], out_weight, preferred_element_type=jnp.float32)
    partner_term = jnp.dot(activated[:, units:], partner_out, preferred_element_type=jnp.float32)
    pair = own_term.astype(jnp.bfloat16).astype(jnp.float32) + partner_term.astype(
        jnp.bfloat16
    ).astype(jnp.float32)
    return scatter_sum(pair.astype(jnp.bfloat16), "tp")


def noise_level(step_value):
    fraction = 1.0 - step_value / STEPS
    return flow_shift * fraction / (1.0 + (flow_shift - 1.0) * fraction)


def shards(
    latent,
    states,
    token_counts,
    text_lens,
    steps_index,
    modulation,
    self_qkv,
    self_out,
    qk_gains,
    cross_query,
    cross_out,
    cross_gain,
    text_kv,
    ffn_in_weight,
    ffn_out_weight,
    head_weight,
):
    row_count = latent.shape[0]
    head_width = HD
    local_cols = self_out.shape[0]
    head_count = local_cols // head_width
    model_width = head_weight.shape[0]
    request_count = token_counts.shape[0]
    tp_parts = lax.axis_size("tp")
    block_rows = row_count * tp_parts
    all_tokens = block_rows * lax.axis_size("req")
    request_ends = jnp.cumsum(token_counts)
    request_range = jnp.arange(request_count, dtype=jnp.int32)
    row_pos = (lax.axis_index("req") * tp_parts + lax.axis_index("tp")) * row_count + jnp.arange(
        row_count, dtype=jnp.int32
    )
    row_onehot = (request_of(row_pos, request_ends)[:, None] == request_range[None, :]).astype(
        jnp.float32
    )
    block_first = lax.axis_index("req") * block_rows
    in_block = jnp.arange(block_rows, dtype=jnp.int32)
    in_block = ((lax.axis_index("tp") + in_block // row_count) % tp_parts) * row_count + (
        in_block % row_count
    )
    query_req = request_of(block_first + in_block, request_ends)
    head_ids = lax.axis_index("tp") * head_count + jnp.arange(head_count, dtype=jnp.int32)
    keep_cols = jnp.repeat((head_ids < HEADS).astype(jnp.float32), head_width)
    hidden_zero = states[0]
    text_local = text_kv[0]
    text_slots = text_local.shape[2]
    text_raw = (
        text_local[:, 0].reshape(request_count * text_slots, local_cols).astype(jnp.float32)
        * keep_cols
    )
    row_mods = jnp.dot(
        row_onehot,
        modulation.reshape(request_count, 6 * model_width),
        precision=lax.Precision.HIGHEST,
    )
    shift_attn = row_mods[:, :model_width]
    scale_attn = row_mods[:, model_width : 2 * model_width]
    gate_attn = row_mods[:, 2 * model_width : 3 * model_width]
    shift_ffn = row_mods[:, 3 * model_width : 4 * model_width]
    scale_ffn = row_mods[:, 4 * model_width : 5 * model_width]
    gate_ffn = row_mods[:, 5 * model_width :]
    normed = (layer_norm(hidden_zero) * (1.0 + scale_attn) + shift_attn).astype(jnp.bfloat16)
    projected = gather_project(normed, self_qkv.reshape(model_width, 3 * local_cols))
    query_raw = projected[:, :local_cols] * keep_cols
    key_raw = projected[:, local_cols : 2 * local_cols] * keep_cols
    row_count_sums = 2 * block_rows
    norm_sums = butterfly_sum(
        jnp.concatenate(
            [
                offset_blocks(
                    jnp.stack(
                        [jnp.sum(query_raw * query_raw, axis=1), jnp.sum(key_raw * key_raw, axis=1)],
                        axis=1,
                    ).reshape(-1),
                    "tp",
                    True,
                ),
                jnp.sum(text_raw * text_raw, axis=1),
            ]
        ),
        "tp",
    )
    row_sums = offset_blocks(norm_sums[:row_count_sums], "tp", False).reshape(block_rows, 2)
    text_sq = norm_sums[row_count_sums:]
    query_sq = row_sums[:, 0]
    key_sq = row_sums[:, 1]
    queries = rms_scale(query_raw, query_sq, model_width, qk_gains[0])
    key_rows = rms_scale(key_raw, key_sq, model_width, qk_gains[1])
    value_rows = projected[:, 2 * local_cols :].astype(jnp.bfloat16)
    kv_all = lax.all_gather(jnp.stack([key_rows, value_rows]), "req", axis=1, tiled=True)
    key_pos = jnp.arange(all_tokens, dtype=jnp.int32)
    key_pos = (key_pos // block_rows) * block_rows + jnp.tile(in_block, lax.axis_size("req"))
    self_num, self_den = attention_sums(
        queries,
        query_req,
        kv_all,
        request_of(key_pos, request_ends),
        head_count,
        head_width,
        key_block,
    )
    self_mix = (self_num / self_den * keep_cols).astype(jnp.bfloat16)
    hidden_one = hidden_zero + gate_attn * scatter_project(self_mix, self_out)
    cross_in = (layer_norm(hidden_one) * cross_gain).astype(jnp.bfloat16)
    cross_raw = gather_project(cross_in, cross_query) * keep_cols
    cross_sq = natural_butterfly(jnp.sum(cross_raw * cross_raw, axis=1), "tp")
    cross_q = rms_scale(cross_raw, cross_sq, model_width, qk_gains[2])
    text_keys = rms_scale(text_raw, text_sq, model_width, qk_gains[3])
    text_values = text_local[:, 1].reshape(request_count * text_slots, local_cols)
    text_req = jnp.repeat(request_range, text_slots)
    text_pos = jnp.tile(jnp.arange(text_slots, dtype=jnp.int32), request_count)
    text_limit = jnp.sum(
        jnp.where(text_req[:, None] == request_range[None, :], text_lens[0][None, :], 0), axis=1
    )
    text_req = jnp.where(text_pos < text_limit, text_req, -1)
    cross_num, cross_den = attention_sums(
        cross_q,
        query_req,
        jnp.stack([text_keys, text_values]),
        text_req,
        head_count,
        head_width,
        text_slots,
    )
    cross_mix = (cross_num / cross_den * keep_cols).astype(jnp.bfloat16)
    hidden_two = hidden_one + scatter_project(cross_mix, cross_out)
    ffn_in = (layer_norm(hidden_two) * (1.0 + scale_ffn) + shift_ffn).astype(jnp.bfloat16)
    hidden_three = hidden_two + gate_ffn * feed_forward(ffn_in, ffn_in_weight, ffn_out_weight)
    velocity_own = jnp.dot(
        layer_norm(hidden_three).astype(jnp.bfloat16),
        head_weight,
        preferred_element_type=jnp.float32,
    )
    velocity_other = swapped(velocity_own, "cfg", 0)
    first_half = lax.axis_index("cfg") == 0
    cond_speed = jnp.where(first_half, velocity_own, velocity_other)
    plain_speed = jnp.where(first_half, velocity_other, velocity_own)
    guided = plain_speed + guide_scale * (cond_speed - plain_speed)
    row_squares = jnp.stack(
        [jnp.sum(cond_speed * cond_speed, axis=1), jnp.sum(guided * guided, axis=1)], axis=1
    )
    square_sums = jnp.dot(jnp.transpose(row_onehot), row_squares, precision=lax.Precision.HIGHEST)
    peak_speed = jnp.max(row_onehot * jnp.max(jnp.abs(guided), axis=1)[:, None], axis=0)
    packed = jnp.concatenate([square_sums.reshape(-1), peak_speed])
    sum_count = 2 * request_count
    for axis in ("tp", "req"):
        for stride, width in reduction_rounds(axis):
            parts = group_exchange(packed, axis, stride, width)
            sums, peaks = parts[0][:sum_count], parts[0][sum_count:]
            for part in parts[1:]:
                sums = sums + part[:sum_count]
                peaks = jnp.maximum(peaks, part[sum_count:])
            packed = jnp.concatenate([sums, peaks])
    square_sums = packed[:sum_count].reshape(request_count, 2)
    peak_speed = packed[sum_count:]
    entry_counts = token_counts.astype(jnp.float32) * guided.shape[1]
    cond_rms = jnp.sqrt(square_sums[:, 0] / entry_counts + stat_eps)
    guided_rms = jnp.sqrt(square_sums[:, 1] / entry_counts + stat_eps)
    factor = rescale_mix * cond_rms / guided_rms + (1.0 - rescale_mix)
    step_value = steps_index.astype(jnp.float32)
    delta_t = noise_level(step_value + 1.0) - noise_level(step_value)
    per_row = jnp.dot(
        row_onehot, jnp.stack([factor, delta_t], axis=1), precision=lax.Precision.HIGHEST
    )
    velocity = per_row[:, 0:1] * guided
    new_latent = latent + per_row[:, 1:2] * velocity
    own_cols = guided.shape[1] // lax.axis_size("cfg")
    col_start = lax.axis_index("cfg") * own_cols
    velocity_part = lax.dynamic_slice_in_dim(velocity, col_start, own_cols, 1)
    latent_part = lax.dynamic_slice_in_dim(new_latent, col_start, own_cols, 1)
    return (latent_part, velocity_part, factor * peak_speed)


def solution(mesh):
    in_specs = (
        P(("req", "tp"), None),
        P("cfg", ("req", "tp"), None),
        P(),
        P("cfg", None),
        P(),
        P(),
        P(None, None, "tp"),
        P("tp", None),
        P(None, "tp"),
        P(None, "tp"),
        P("tp", None),
        P(),
        P("cfg", None, None, None, "tp"),
        P(("cfg", "tp"), None),
        P(("cfg", "tp"), None),
        P(),
    )
    out_specs = (P(("req", "tp"), "cfg"), P(("req", "tp"), "cfg"), P())
    return jax.shard_map(shards, mesh=mesh, in_specs=in_specs, out_specs=out_specs, check_vma=False)
```

```python
import jax
import jax.numpy as jnp
import functools
from jax import lax
from jax.experimental import pallas as pl
from jax.sharding import PartitionSpec as P

HEADS = 12
HD = 128
STEPS = 50


key_block = 1024
guide_scale = 5.0
rescale_mix = 0.7
flow_shift = 5.0
norm_eps = 1e-06
stat_eps = 1e-05


def swapped(value, axis, stride):
    mask = 2**stride
    pairs = [(source, source ^ mask) for source in range(lax.axis_size(axis))]
    return lax.ppermute(value, axis, pairs)


def shifted(value, axis, step):
    size = lax.axis_size(axis)
    return lax.ppermute(value, axis, [(source, (source + step) % size) for source in range(size)])


def ring_gather(value, axis):
    size = lax.axis_size(axis)
    forward, backward = value, value
    ahead, behind = [], []
    for unused in range(size // 2):
        forward = shifted(forward, axis, 1)
        behind.append(forward)
    for unused in range((size - 1) // 2):
        backward = shifted(backward, axis, -1)
        ahead.append(backward)
    return jnp.concatenate([value] + ahead + behind[::-1], axis=0)


def scatter_sum(value, axis):
    size = lax.axis_size(axis)
    rows = value.shape[0] // size
    total = value[:rows].astype(jnp.float32)
    for step in range(1, size):
        outgoing = value[step * rows : (step + 1) * rows]
        total = total + shifted(outgoing, axis, step).astype(jnp.float32)
    return total


def offset_blocks(value, axis, to_natural):
    size = lax.axis_size(axis)
    me = lax.axis_index(axis)
    blocks = value.reshape(size, value.shape[0] // size)
    doubled = jnp.concatenate([blocks, blocks], axis=0)
    start = (size - me) % size if to_natural else me
    return lax.dynamic_slice_in_dim(doubled, start, size, axis=0).reshape(value.shape)


def natural_butterfly(row_values, axis):
    natural = offset_blocks(row_values, axis, True)
    return offset_blocks(butterfly_sum(natural, axis), axis, False)


def butterfly_sum(value, axis):
    stride = 1
    while stride < lax.axis_size(axis):
        value = value + swapped(value, axis, stride.bit_length() - 1)
        stride *= 2
    return value


def layer_norm(values):
    average = jnp.mean(values, axis=-1, keepdims=True)
    centered = values - average
    spread = jnp.mean(centered * centered, axis=-1, keepdims=True)
    return centered * lax.rsqrt(spread + norm_eps)


def rms_scale(values, square_sum, width, gains):
    return (values * lax.rsqrt(square_sum / width + norm_eps)[:, None] * gains).astype(jnp.bfloat16)


def request_of(positions, request_ends):
    return jnp.sum((positions[:, None] >= request_ends[None, :]).astype(jnp.int32), axis=1)


def attention_body(head_count, head_width, q_ref, k_ref, v_ref, qreq_ref, kreq_ref, num_ref, den_ref):
    @pl.when(pl.program_id(0) == 0)
    def _():
        num_ref[...] = jnp.zeros_like(num_ref)
        den_ref[...] = jnp.zeros_like(den_ref)

    same_req = qreq_ref[...] == kreq_ref[...]
    for head in range(head_count):
        cols = slice(head * head_width, (head + 1) * head_width)
        scores = lax.dot_general(
            q_ref[:, cols], k_ref[:, cols], (((1,), (1,)), ((), ())), preferred_element_type=jnp.float32
        ) * head_width ** (-0.5)
        weights = jnp.where(same_req, jnp.exp(scores), 0.0)
        num_ref[:, cols] += jnp.dot(
            weights.astype(jnp.bfloat16), v_ref[:, cols], preferred_element_type=jnp.float32
        )
        den_ref[:, cols] += jnp.broadcast_to(jnp.sum(weights, axis=1, keepdims=True), (weights.shape[0], head_width))


def attention_sums(queries, query_req, key_value, key_req, head_count, head_width, key_block):
    query_count, width = queries.shape
    key_count = key_value.shape[1]
    steps = key_count // key_block
    flops = 4 * query_count * key_count * width
    return pl.pallas_call(
        functools.partial(attention_body, head_count, head_width),
        grid=(steps,),
        in_specs=[
            pl.BlockSpec((query_count, width), lambda j: (0, 0)),
            pl.BlockSpec((None, key_block, width), lambda j: (0, j, 0)),
            pl.BlockSpec((None, key_block, width), lambda j: (1, j, 0)),
            pl.BlockSpec((query_count, 1), lambda j: (0, 0)),
            pl.BlockSpec((1, key_block), lambda j: (0, j)),
        ],
        out_specs=[
            pl.BlockSpec((query_count, width), lambda j: (0, 0)),
            pl.BlockSpec((query_count, width), lambda j: (0, 0)),
        ],
        out_shape=[
            jax.ShapeDtypeStruct((query_count, width), jnp.float32),
            jax.ShapeDtypeStruct((query_count, width), jnp.float32),
        ],
        cost_estimate=pl.CostEstimate(
            flops=flops,
            transcendentals=query_count * key_count * head_count,
            bytes_accessed=2 * (query_count + 2 * key_count) * width + 8 * query_count * width,
        ),
    )(queries, key_value, key_value, query_req.reshape(query_count, 1), key_req.reshape(1, key_count))


def gather_project(row_block, weight):
    return jnp.dot(ring_gather(row_block, "tp"), weight, preferred_element_type=jnp.float32)


def scatter_project(mixed, weight):
    return scatter_sum(
        jnp.dot(mixed, weight, preferred_element_type=jnp.float32).astype(jnp.bfloat16), "tp"
    )


def feed_forward(ffn_rows, in_weight, out_weight, partner_in, partner_out):
    units = in_weight.shape[0]
    rows = ring_gather(ffn_rows, "tp")
    up_part = lax.dot_general(
        rows,
        jnp.concatenate([in_weight, partner_in], axis=0),
        (((1,), (1,)), ((), ())),
        preferred_element_type=jnp.float32,
    )
    activated = jax.nn.gelu(up_part, approximate=True).astype(jnp.bfloat16)
    own_term = jnp.dot(activated[:, :units], out_weight, preferred_element_type=jnp.float32)
    partner_term = jnp.dot(activated[:, units:], partner_out, preferred_element_type=jnp.float32)
    pair = own_term.astype(jnp.bfloat16).astype(jnp.float32) + partner_term.astype(
        jnp.bfloat16
    ).astype(jnp.float32)
    return scatter_sum(pair.astype(jnp.bfloat16), "tp")


def noise_level(step_value):
    fraction = 1.0 - step_value / STEPS
    return flow_shift * fraction / (1.0 + (flow_shift - 1.0) * fraction)


def shards(
    latent,
    states,
    token_counts,
    text_lens,
    steps_index,
    modulation,
    self_qkv,
    self_out,
    qk_gains,
    cross_query,
    cross_out,
    cross_gain,
    text_kv,
    ffn_in_weight,
    ffn_out_weight,
    head_weight,
):
    row_count = latent.shape[0]
    head_width = HD
    local_cols = self_out.shape[0]
    head_count = local_cols // head_width
    model_width = head_weight.shape[0]
    request_count = token_counts.shape[0]
    tp_parts = lax.axis_size("tp")
    block_rows = row_count * tp_parts
    all_tokens = block_rows * lax.axis_size("req")
    request_ends = jnp.cumsum(token_counts)
    request_range = jnp.arange(request_count, dtype=jnp.int32)
    row_pos = (lax.axis_index("req") * tp_parts + lax.axis_index("tp")) * row_count + jnp.arange(
        row_count, dtype=jnp.int32
    )
    row_onehot = (request_of(row_pos, request_ends)[:, None] == request_range[None, :]).astype(
        jnp.float32
    )
    block_first = lax.axis_index("req") * block_rows
    in_block = jnp.arange(block_rows, dtype=jnp.int32)
    in_block = ((lax.axis_index("tp") + in_block // row_count) % tp_parts) * row_count + (
        in_block % row_count
    )
    query_req = request_of(block_first + in_block, request_ends)
    head_ids = lax.axis_index("tp") * head_count + jnp.arange(head_count, dtype=jnp.int32)
    keep_cols = jnp.repeat((head_ids < HEADS).astype(jnp.float32), head_width)
    hidden_zero = states[0]
    text_local = text_kv[0]
    text_slots = text_local.shape[2]
    text_raw = (
        text_local[:, 0].reshape(request_count * text_slots, local_cols).astype(jnp.float32)
        * keep_cols
    )
    row_mods = jnp.dot(
        row_onehot,
        modulation.reshape(request_count, 6 * model_width),
        precision=lax.Precision.HIGHEST,
    )
    shift_attn = row_mods[:, :model_width]
    scale_attn = row_mods[:, model_width : 2 * model_width]
    gate_attn = row_mods[:, 2 * model_width : 3 * model_width]
    shift_ffn = row_mods[:, 3 * model_width : 4 * model_width]
    scale_ffn = row_mods[:, 4 * model_width : 5 * model_width]
    gate_ffn = row_mods[:, 5 * model_width :]
    normed = (layer_norm(hidden_zero) * (1.0 + scale_attn) + shift_attn).astype(jnp.bfloat16)
    projected = gather_project(normed, self_qkv.reshape(model_width, 3 * local_cols))
    query_raw = projected[:, :local_cols] * keep_cols
    key_raw = projected[:, local_cols : 2 * local_cols] * keep_cols
    row_count_sums = 2 * block_rows
    norm_sums = butterfly_sum(
        jnp.concatenate(
            [
                offset_blocks(
                    jnp.stack(
                        [jnp.sum(query_raw * query_raw, axis=1), jnp.sum(key_raw * key_raw, axis=1)],
                        axis=1,
                    ).reshape(-1),
                    "tp",
                    True,
                ),
                jnp.sum(text_raw * text_raw, axis=1),
            ]
        ),
        "tp",
    )
    row_sums = offset_blocks(norm_sums[:row_count_sums], "tp", False).reshape(block_rows, 2)
    text_sq = norm_sums[row_count_sums:]
    query_sq = row_sums[:, 0]
    key_sq = row_sums[:, 1]
    queries = rms_scale(query_raw, query_sq, model_width, qk_gains[0])
    key_rows = rms_scale(key_raw, key_sq, model_width, qk_gains[1])
    value_rows = projected[:, 2 * local_cols :].astype(jnp.bfloat16)
    kv_all = lax.all_gather(jnp.stack([key_rows, value_rows]), "req", axis=1, tiled=True)
    partner_weights, kv_all = lax.optimization_barrier(
        (swapped((ffn_in_weight, ffn_out_weight), "cfg", 0), kv_all)
    )
    key_pos = jnp.arange(all_tokens, dtype=jnp.int32)
    key_pos = (key_pos // block_rows) * block_rows + jnp.tile(in_block, lax.axis_size("req"))
    self_num, self_den = attention_sums(
        queries,
        query_req,
        kv_all,
        request_of(key_pos, request_ends),
        head_count,
        head_width,
        key_block,
    )
    self_mix = (self_num / self_den * keep_cols).astype(jnp.bfloat16)
    hidden_one = hidden_zero + gate_attn * scatter_project(self_mix, self_out)
    cross_in = (layer_norm(hidden_one) * cross_gain).astype(jnp.bfloat16)
    cross_raw = gather_project(cross_in, cross_query) * keep_cols
    cross_sq = natural_butterfly(jnp.sum(cross_raw * cross_raw, axis=1), "tp")
    cross_q = rms_scale(cross_raw, cross_sq, model_width, qk_gains[2])
    text_keys = rms_scale(text_raw, text_sq, model_width, qk_gains[3])
    text_values = text_local[:, 1].reshape(request_count * text_slots, local_cols)
    text_req = jnp.repeat(request_range, text_slots)
    text_pos = jnp.tile(jnp.arange(text_slots, dtype=jnp.int32), request_count)
    text_limit = jnp.sum(
        jnp.where(text_req[:, None] == request_range[None, :], text_lens[0][None, :], 0), axis=1
    )
    text_req = jnp.where(text_pos < text_limit, text_req, -1)
    cross_num, cross_den = attention_sums(
        cross_q,
        query_req,
        jnp.stack([text_keys, text_values]),
        text_req,
        head_count,
        head_width,
        text_slots,
    )
    cross_mix = (cross_num / cross_den * keep_cols).astype(jnp.bfloat16)
    hidden_two = hidden_one + scatter_project(cross_mix, cross_out)
    ffn_in = (layer_norm(hidden_two) * (1.0 + scale_ffn) + shift_ffn).astype(jnp.bfloat16)
    hidden_three = hidden_two + gate_ffn * feed_forward(ffn_in, ffn_in_weight, ffn_out_weight, *partner_weights)
    velocity_own = jnp.dot(
        layer_norm(hidden_three).astype(jnp.bfloat16),
        head_weight,
        preferred_element_type=jnp.float32,
    )
    velocity_other = swapped(velocity_own, "cfg", 0)
    first_half = lax.axis_index("cfg") == 0
    cond_speed = jnp.where(first_half, velocity_own, velocity_other)
    plain_speed = jnp.where(first_half, velocity_other, velocity_own)
    guided = plain_speed + guide_scale * (cond_speed - plain_speed)
    row_squares = jnp.stack(
        [jnp.sum(cond_speed * cond_speed, axis=1), jnp.sum(guided * guided, axis=1)], axis=1
    )
    square_sums = jnp.dot(jnp.transpose(row_onehot), row_squares, precision=lax.Precision.HIGHEST)
    peak_speed = jnp.max(row_onehot * jnp.max(jnp.abs(guided), axis=1)[:, None], axis=0)
    packed = jnp.concatenate([square_sums.reshape(-1), peak_speed])
    sum_count = 2 * request_count
    for axis in ("tp", "req"):
        stride = 1
        while stride < lax.axis_size(axis):
            other = swapped(packed, axis, stride.bit_length() - 1)
            packed = jnp.concatenate(
                [packed[:sum_count] + other[:sum_count], jnp.maximum(packed[sum_count:], other[sum_count:])]
            )
            stride *= 2
    square_sums = packed[:sum_count].reshape(request_count, 2)
    peak_speed = packed[sum_count:]
    entry_counts = token_counts.astype(jnp.float32) * guided.shape[1]
    cond_rms = jnp.sqrt(square_sums[:, 0] / entry_counts + stat_eps)
    guided_rms = jnp.sqrt(square_sums[:, 1] / entry_counts + stat_eps)
    factor = rescale_mix * cond_rms / guided_rms + (1.0 - rescale_mix)
    step_value = steps_index.astype(jnp.float32)
    delta_t = noise_level(step_value + 1.0) - noise_level(step_value)
    per_row = jnp.dot(
        row_onehot, jnp.stack([factor, delta_t], axis=1), precision=lax.Precision.HIGHEST
    )
    velocity = per_row[:, 0:1] * guided
    new_latent = latent + per_row[:, 1:2] * velocity
    own_cols = guided.shape[1] // lax.axis_size("cfg")
    col_start = lax.axis_index("cfg") * own_cols
    velocity_part = lax.dynamic_slice_in_dim(velocity, col_start, own_cols, 1)
    latent_part = lax.dynamic_slice_in_dim(new_latent, col_start, own_cols, 1)
    return (latent_part, velocity_part, factor * peak_speed)


def solution(mesh):
    in_specs = (
        P(("req", "tp"), None),
        P("cfg", ("req", "tp"), None),
        P(),
        P("cfg", None),
        P(),
        P(),
        P(None, None, "tp"),
        P("tp", None),
        P(None, "tp"),
        P(None, "tp"),
        P("tp", None),
        P(),
        P("cfg", None, None, None, "tp"),
        P(("cfg", "tp"), None),
        P(("cfg", "tp"), None),
        P(),
    )
    out_specs = (P(("req", "tp"), "cfg"), P(("req", "tp"), "cfg"), P())
    return jax.shard_map(shards, mesh=mesh, in_specs=in_specs, out_specs=out_specs, check_vma=False)
```

```python
import jax
import jax.numpy as jnp
import functools
from jax import lax
from jax.experimental import pallas as pl
from jax.sharding import PartitionSpec as P

HEADS = 12
HD = 128
STEPS = 50


key_block = 2048
guide_scale = 5.0
rescale_mix = 0.7
flow_shift = 5.0
norm_eps = 1e-06
stat_eps = 1e-05


def swapped(value, axis, stride):
    mask = 2**stride
    pairs = [(source, source ^ mask) for source in range(lax.axis_size(axis))]
    return lax.ppermute(value, axis, pairs)


def shifted(value, axis, step):
    size = lax.axis_size(axis)
    return lax.ppermute(value, axis, [(source, (source + step) % size) for source in range(size)])


def ring_gather(value, axis):
    size = lax.axis_size(axis)
    forward, backward = value, value
    ahead, behind = [], []
    for unused in range(size // 2):
        forward = shifted(forward, axis, 1)
        behind.append(forward)
    for unused in range((size - 1) // 2):
        backward = shifted(backward, axis, -1)
        ahead.append(backward)
    return jnp.concatenate([value] + ahead + behind[::-1], axis=0)


def scatter_sum(value, axis):
    size = lax.axis_size(axis)
    rows = value.shape[0] // size
    total = value[:rows].astype(jnp.float32)
    for step in range(1, size):
        outgoing = value[step * rows : (step + 1) * rows]
        total = total + shifted(outgoing, axis, step).astype(jnp.float32)
    return total


def offset_blocks(value, axis, to_natural):
    size = lax.axis_size(axis)
    me = lax.axis_index(axis)
    blocks = value.reshape(size, value.shape[0] // size)
    doubled = jnp.concatenate([blocks, blocks], axis=0)
    start = (size - me) % size if to_natural else me
    return lax.dynamic_slice_in_dim(doubled, start, size, axis=0).reshape(value.shape)


def natural_butterfly(row_values, axis):
    natural = offset_blocks(row_values, axis, True)
    return offset_blocks(butterfly_sum(natural, axis), axis, False)


def butterfly_sum(value, axis):
    stride = 1
    while stride < lax.axis_size(axis):
        value = value + swapped(value, axis, stride.bit_length() - 1)
        stride *= 2
    return value


def layer_norm(values):
    average = jnp.mean(values, axis=-1, keepdims=True)
    centered = values - average
    spread = jnp.mean(centered * centered, axis=-1, keepdims=True)
    return centered * lax.rsqrt(spread + norm_eps)


def rms_scale(values, square_sum, width, gains):
    return (values * lax.rsqrt(square_sum / width + norm_eps)[:, None] * gains).astype(jnp.bfloat16)


def request_of(positions, request_ends):
    return jnp.sum((positions[:, None] >= request_ends[None, :]).astype(jnp.int32), axis=1)


def attention_body(head_count, head_width, q_ref, k_ref, v_ref, qreq_ref, kreq_ref, num_ref, den_ref):
    @pl.when(pl.program_id(0) == 0)
    def _():
        num_ref[...] = jnp.zeros_like(num_ref)
        den_ref[...] = jnp.zeros_like(den_ref)

    same_req = qreq_ref[...] == kreq_ref[...]
    for head in range(head_count):
        cols = slice(head * head_width, (head + 1) * head_width)
        scores = lax.dot_general(
            q_ref[:, cols], k_ref[:, cols], (((1,), (1,)), ((), ())), preferred_element_type=jnp.float32
        ) * head_width ** (-0.5)
        weights = jnp.where(same_req, jnp.exp(scores), 0.0)
        num_ref[:, cols] += jnp.dot(
            weights.astype(jnp.bfloat16), v_ref[:, cols], preferred_element_type=jnp.float32
        )
        den_ref[:, cols] += jnp.broadcast_to(jnp.sum(weights, axis=1, keepdims=True), (weights.shape[0], head_width))


def attention_sums(queries, query_req, key_value, key_req, head_count, head_width, key_block):
    query_count, width = queries.shape
    key_count = key_value.shape[1]
    steps = key_count // key_block
    flops = 4 * query_count * key_count * width
    return pl.pallas_call(
        functools.partial(attention_body, head_count, head_width),
        grid=(steps,),
        in_specs=[
            pl.BlockSpec((query_count, width), lambda j: (0, 0)),
            pl.BlockSpec((None, key_block, width), lambda j: (0, j, 0)),
            pl.BlockSpec((None, key_block, width), lambda j: (1, j, 0)),
            pl.BlockSpec((query_count, 1), lambda j: (0, 0)),
            pl.BlockSpec((1, key_block), lambda j: (0, j)),
        ],
        out_specs=[
            pl.BlockSpec((query_count, width), lambda j: (0, 0)),
            pl.BlockSpec((query_count, width), lambda j: (0, 0)),
        ],
        out_shape=[
            jax.ShapeDtypeStruct((query_count, width), jnp.float32),
            jax.ShapeDtypeStruct((query_count, width), jnp.float32),
        ],
        cost_estimate=pl.CostEstimate(
            flops=flops,
            transcendentals=query_count * key_count * head_count,
            bytes_accessed=2 * (query_count + 2 * key_count) * width + 8 * query_count * width,
        ),
    )(queries, key_value, key_value, query_req.reshape(query_count, 1), key_req.reshape(1, key_count))


def gather_project(row_block, weight):
    return jnp.dot(ring_gather(row_block, "tp"), weight, preferred_element_type=jnp.float32)


def scatter_project(mixed, weight):
    return scatter_sum(
        jnp.dot(mixed, weight, preferred_element_type=jnp.float32).astype(jnp.bfloat16), "tp"
    )


def feed_forward(ffn_rows, in_weight, out_weight):
    partner_in, partner_out = swapped((in_weight, out_weight), "cfg", 0)
    units = in_weight.shape[0]
    rows = ring_gather(ffn_rows, "tp")
    up_part = lax.dot_general(
        rows,
        jnp.concatenate([in_weight, partner_in], axis=0),
        (((1,), (1,)), ((), ())),
        preferred_element_type=jnp.float32,
    )
    activated = jax.nn.gelu(up_part, approximate=True).astype(jnp.bfloat16)
    own_term = jnp.dot(activated[:, :units], out_weight, preferred_element_type=jnp.float32)
    partner_term = jnp.dot(activated[:, units:], partner_out, preferred_element_type=jnp.float32)
    pair = own_term.astype(jnp.bfloat16).astype(jnp.float32) + partner_term.astype(
        jnp.bfloat16
    ).astype(jnp.float32)
    return scatter_sum(pair.astype(jnp.bfloat16), "tp")


def noise_level(step_value):
    fraction = 1.0 - step_value / STEPS
    return flow_shift * fraction / (1.0 + (flow_shift - 1.0) * fraction)


def shards(
    latent,
    states,
    token_counts,
    text_lens,
    steps_index,
    modulation,
    self_qkv,
    self_out,
    qk_gains,
    cross_query,
    cross_out,
    cross_gain,
    text_kv,
    ffn_in_weight,
    ffn_out_weight,
    head_weight,
):
    row_count = latent.shape[0]
    head_width = HD
    local_cols = self_out.shape[0]
    head_count = local_cols // head_width
    model_width = head_weight.shape[0]
    request_count = token_counts.shape[0]
    tp_parts = lax.axis_size("tp")
    block_rows = row_count * tp_parts
    all_tokens = block_rows * lax.axis_size("req")
    request_ends = jnp.cumsum(token_counts)
    request_range = jnp.arange(request_count, dtype=jnp.int32)
    row_pos = (lax.axis_index("req") * tp_parts + lax.axis_index("tp")) * row_count + jnp.arange(
        row_count, dtype=jnp.int32
    )
    row_onehot = (request_of(row_pos, request_ends)[:, None] == request_range[None, :]).astype(
        jnp.float32
    )
    block_first = lax.axis_index("req") * block_rows
    in_block = jnp.arange(block_rows, dtype=jnp.int32)
    in_block = ((lax.axis_index("tp") + in_block // row_count) % tp_parts) * row_count + (
        in_block % row_count
    )
    query_req = request_of(block_first + in_block, request_ends)
    head_ids = lax.axis_index("tp") * head_count + jnp.arange(head_count, dtype=jnp.int32)
    keep_cols = jnp.repeat((head_ids < HEADS).astype(jnp.float32), head_width)
    hidden_zero = states[0]
    text_local = text_kv[0]
    text_slots = text_local.shape[2]
    text_raw = (
        text_local[:, 0].reshape(request_count * text_slots, local_cols).astype(jnp.float32)
        * keep_cols
    )
    row_mods = jnp.dot(
        row_onehot,
        modulation.reshape(request_count, 6 * model_width),
        precision=lax.Precision.HIGHEST,
    )
    shift_attn = row_mods[:, :model_width]
    scale_attn = row_mods[:, model_width : 2 * model_width]
    gate_attn = row_mods[:, 2 * model_width : 3 * model_width]
    shift_ffn = row_mods[:, 3 * model_width : 4 * model_width]
    scale_ffn = row_mods[:, 4 * model_width : 5 * model_width]
    gate_ffn = row_mods[:, 5 * model_width :]
    normed = (layer_norm(hidden_zero) * (1.0 + scale_attn) + shift_attn).astype(jnp.bfloat16)
    projected = gather_project(normed, self_qkv.reshape(model_width, 3 * local_cols))
    query_raw = projected[:, :local_cols] * keep_cols
    key_raw = projected[:, local_cols : 2 * local_cols] * keep_cols
    row_count_sums = 2 * block_rows
    norm_sums = butterfly_sum(
        jnp.concatenate(
            [
                offset_blocks(
                    jnp.stack(
                        [jnp.sum(query_raw * query_raw, axis=1), jnp.sum(key_raw * key_raw, axis=1)],
                        axis=1,
                    ).reshape(-1),
                    "tp",
                    True,
                ),
                jnp.sum(text_raw * text_raw, axis=1),
            ]
        ),
        "tp",
    )
    row_sums = offset_blocks(norm_sums[:row_count_sums], "tp", False).reshape(block_rows, 2)
    text_sq = norm_sums[row_count_sums:]
    query_sq = row_sums[:, 0]
    key_sq = row_sums[:, 1]
    queries = rms_scale(query_raw, query_sq, model_width, qk_gains[0])
    key_rows = rms_scale(key_raw, key_sq, model_width, qk_gains[1])
    value_rows = projected[:, 2 * local_cols :].astype(jnp.bfloat16)
    kv_all = lax.all_gather(jnp.stack([key_rows, value_rows]), "req", axis=1, tiled=True)
    key_pos = jnp.arange(all_tokens, dtype=jnp.int32)
    key_pos = (key_pos // block_rows) * block_rows + jnp.tile(in_block, lax.axis_size("req"))
    self_num, self_den = attention_sums(
        queries,
        query_req,
        kv_all,
        request_of(key_pos, request_ends),
        head_count,
        head_width,
        key_block,
    )
    self_mix = (self_num / self_den * keep_cols).astype(jnp.bfloat16)
    hidden_one = hidden_zero + gate_attn * scatter_project(self_mix, self_out)
    cross_in = (layer_norm(hidden_one) * cross_gain).astype(jnp.bfloat16)
    cross_raw = gather_project(cross_in, cross_query) * keep_cols
    cross_sq = natural_butterfly(jnp.sum(cross_raw * cross_raw, axis=1), "tp")
    cross_q = rms_scale(cross_raw, cross_sq, model_width, qk_gains[2])
    text_keys = rms_scale(text_raw, text_sq, model_width, qk_gains[3])
    text_values = text_local[:, 1].reshape(request_count * text_slots, local_cols)
    text_req = jnp.repeat(request_range, text_slots)
    text_pos = jnp.tile(jnp.arange(text_slots, dtype=jnp.int32), request_count)
    text_limit = jnp.sum(
        jnp.where(text_req[:, None] == request_range[None, :], text_lens[0][None, :], 0), axis=1
    )
    text_req = jnp.where(text_pos < text_limit, text_req, -1)
    cross_num, cross_den = attention_sums(
        cross_q,
        query_req,
        jnp.stack([text_keys, text_values]),
        text_req,
        head_count,
        head_width,
        request_count * text_slots,
    )
    cross_mix = (cross_num / cross_den * keep_cols).astype(jnp.bfloat16)
    hidden_two = hidden_one + scatter_project(cross_mix, cross_out)
    ffn_in = (layer_norm(hidden_two) * (1.0 + scale_ffn) + shift_ffn).astype(jnp.bfloat16)
    hidden_three = hidden_two + gate_ffn * feed_forward(ffn_in, ffn_in_weight, ffn_out_weight)
    velocity_own = jnp.dot(
        layer_norm(hidden_three).astype(jnp.bfloat16),
        head_weight,
        preferred_element_type=jnp.float32,
    )
    velocity_other = swapped(velocity_own, "cfg", 0)
    first_half = lax.axis_index("cfg") == 0
    cond_speed = jnp.where(first_half, velocity_own, velocity_other)
    plain_speed = jnp.where(first_half, velocity_other, velocity_own)
    guided = plain_speed + guide_scale * (cond_speed - plain_speed)
    row_squares = jnp.stack(
        [jnp.sum(cond_speed * cond_speed, axis=1), jnp.sum(guided * guided, axis=1)], axis=1
    )
    square_sums = jnp.dot(jnp.transpose(row_onehot), row_squares, precision=lax.Precision.HIGHEST)
    peak_speed = jnp.max(row_onehot * jnp.max(jnp.abs(guided), axis=1)[:, None], axis=0)
    packed = jnp.concatenate([square_sums.reshape(-1), peak_speed])
    sum_count = 2 * request_count
    for axis in ("tp", "req"):
        stride = 1
        while stride < lax.axis_size(axis):
            other = swapped(packed, axis, stride.bit_length() - 1)
            packed = jnp.concatenate(
                [packed[:sum_count] + other[:sum_count], jnp.maximum(packed[sum_count:], other[sum_count:])]
            )
            stride *= 2
    square_sums = packed[:sum_count].reshape(request_count, 2)
    peak_speed = packed[sum_count:]
    entry_counts = token_counts.astype(jnp.float32) * guided.shape[1]
    cond_rms = jnp.sqrt(square_sums[:, 0] / entry_counts + stat_eps)
    guided_rms = jnp.sqrt(square_sums[:, 1] / entry_counts + stat_eps)
    factor = rescale_mix * cond_rms / guided_rms + (1.0 - rescale_mix)
    step_value = steps_index.astype(jnp.float32)
    delta_t = noise_level(step_value + 1.0) - noise_level(step_value)
    per_row = jnp.dot(
        row_onehot, jnp.stack([factor, delta_t], axis=1), precision=lax.Precision.HIGHEST
    )
    velocity = per_row[:, 0:1] * guided
    new_latent = latent + per_row[:, 1:2] * velocity
    own_cols = guided.shape[1] // lax.axis_size("cfg")
    col_start = lax.axis_index("cfg") * own_cols
    velocity_part = lax.dynamic_slice_in_dim(velocity, col_start, own_cols, 1)
    latent_part = lax.dynamic_slice_in_dim(new_latent, col_start, own_cols, 1)
    return (latent_part, velocity_part, factor * peak_speed)


def solution(mesh):
    in_specs = (
        P(("req", "tp"), None),
        P("cfg", ("req", "tp"), None),
        P(),
        P("cfg", None),
        P(),
        P(),
        P(None, None, "tp"),
        P("tp", None),
        P(None, "tp"),
        P(None, "tp"),
        P("tp", None),
        P(),
        P("cfg", None, None, None, "tp"),
        P(("cfg", "tp"), None),
        P(("cfg", "tp"), None),
        P(),
    )
    out_specs = (P(("req", "tp"), "cfg"), P(("req", "tp"), "cfg"), P())
    return jax.shard_map(shards, mesh=mesh, in_specs=in_specs, out_specs=out_specs, check_vma=False)
```
